32 devices in a mesh: shot: 4 (over y, core), tile: 8 (over z, x).
Axes of the slice: x: 2, y: 2, z: 4, core: 2. Of those that a mesh axis runs over, the one named last changes fastest.
Arguments:
- coefs: float32 [3, 16, 1024, 128], P(None, 'shot', 'tile')
- fwd_state: float32 [4, 4, 16, 1024, 128], P('shot', None, None, 'tile'), may hold values from -3 to 3
- adj_state: float32 [4, 4, 16, 1024, 128], P('shot', None, None, 'tile'), may hold values from -3 to 3
- src_cell: int32 [4, 8], P('shot', 'tile'), may hold values from 0 to 262143
- src_wave: float32 [4, 6], P('shot'), may hold values from -8 to 8
- rec_cells: int32 [4, 1024], P('shot', 'tile'), may hold values from 0 to 262143
- observed: float32 [4, 6, 1024], P('shot', None, 'tile'), may hold values from -6 to 6
Outputs:
- gradient: float32 [3, 16, 1024, 128], P(None, 'shot', 'tile')
- fwd_final: float32 [4, 2, 16, 1024, 128], P('shot', None, None, 'tile')
- adj_final: float32 [4, 2, 16, 1024, 128], P('shot', None, None, 'tile')
The draws below stay inside these ranges and needn't reach their ends.
Inputs may be any that keep to these rules, and one draw needn't show every extreme that they name: `src_cell`: local cell index depth * 128 * 128 + first * 128 + second inside the aperture tile. `rec_cells`: local cell index inside the tile of the receiver's block; cells may repeat.
All inputs are finite; a program needn't handle non-finite values.
Results may differ from the reference program's by a relative error of at most 0.0003.
Values sent between devices are 32-bit elements; how exact they have to be, the bound alone decides.
No kernel may reach another device: no remote copies, remote signals or barrier semaphores. Data moves between devices by JAX's collectives and lax.ppermute only.
A program may use at most 192 MiB of HBM per device.

```python
import jax
import jax.numpy as jnp
from jax import lax

AX = 128
AY = 128
AZ = 16
STEPS = 6
NREC = 128
NX = 1024
N_SHOT = 4
N_TILE = 8


def draw_coefs(key, part):
    shape = (AZ, AX * N_TILE, AY)
    keys = jax.random.split(jax.random.fold_in(key, 17), 3)
    speed = jax.random.uniform(keys[0], shape, jnp.float32, 0.03, 0.15)
    stretch = jax.random.uniform(keys[1], shape, jnp.float32, 1.2, 1.6)
    couple = jax.random.uniform(keys[2], shape, jnp.float32, 0.9, 1.05)
    return jnp.stack([speed, stretch, couple])


def touch_ends(result, rng, low, top_value):
    dims = result.shape
    place = [jax.random.randint(jax.random.fold_in(rng, axis), (), 0, dims[axis]) for axis in range(len(dims))]
    result = result.at[tuple(place)].set(low)
    longest = dims.index(max(dims))
    place[longest] = (place[longest] + 1) % dims[longest]
    return result.at[tuple(place)].set(top_value)


def block_levels(rng, dims, pieces, low, largest):
    def one(axis_at, parts):
        draws = jax.random.uniform(jax.random.fold_in(jax.random.fold_in(rng, 6), axis_at), (parts,), jnp.float32, low / len(pieces), largest / len(pieces))
        return jnp.repeat(jnp.exp(draws), dims[axis_at] // parts).reshape((-1,) + (1,) * (len(dims) - axis_at - 1))

    loudness = one(*pieces[0])
    for cut in pieces[1:]:
        loudness = loudness * one(*cut)
    return loudness


def gaussian(own_key, dims, scale, most, cuts=(), kind=jnp.bfloat16):
    level = block_levels(own_key, dims, cuts, -0.22, 0.18) if cuts else 1.0
    drawn = jax.random.normal(own_key, dims, jnp.float32) * scale * level
    return jnp.minimum(jnp.maximum(drawn, -most), most).astype(kind)


def setup_inputs(seed: int = 0) -> dict:
    key_of = jax.random.split(jax.random.key(seed), 8)
    return {
        "coefs": draw_coefs(jax.random.fold_in(key_of[7], 71), 0),
        "fwd_state": gaussian(key_of[1], (N_SHOT, 4, AZ, NX, AY), 0.5, 3.0, ((0, 4), (3, 8)), jnp.float32),
        "adj_state": gaussian(key_of[2], (N_SHOT, 4, AZ, NX, AY), 0.5, 3.0, ((0, 4), (3, 8)), jnp.float32),
        "src_cell": touch_ends(jax.random.randint(key_of[3], (N_SHOT, N_TILE), 0, AZ * AX * AY), jax.random.fold_in(key_of[3], 1), 0, (AZ * AX * AY) - 1).astype(jnp.int32),
        "src_wave": gaussian(key_of[4], (N_SHOT, STEPS), 2.0, 8.0, ((0, 4),), jnp.float32),
        "rec_cells": touch_ends(jax.random.randint(key_of[5], (N_SHOT, N_TILE * NREC), 0, AZ * AX * AY), jax.random.fold_in(key_of[5], 1), 0, (AZ * AX * AY) - 1).astype(jnp.int32),
        "observed": gaussian(key_of[6], (N_SHOT, STEPS, N_TILE * NREC), 1.0, 6.0, ((0, 4), (2, 8)), jnp.float32),
    }


def second_diff(field, axis):
    pads = [(0, 0), (0, 0), (0, 0)]
    pads[axis] = (2, 2)
    padded = jnp.pad(field, pads)
    size = field.shape[axis]

    def part(k):
        return lax.slice_in_dim(padded, k, k + size, axis=axis)

    return (-part(0) + 16.0 * part(1) - 30.0 * part(2) + 16.0 * part(3) - part(4)) / 12.0


def global_index(local, tile_of):
    depth = local // (AX * AY)
    first = tile_of * AX + (local // AY) % AX
    second = local % AY
    return ((depth * NX + first) * AY + second).astype(jnp.int32)


def reference(coefs, fwd_state, adj_state, src_cell, src_wave, rec_cells, observed):
    speed, stretch, couple = coefs[0], coefs[1], coefs[2]
    shape = speed.shape
    cells = AZ * NX * AY
    tiles_src = jnp.arange(N_TILE, dtype=jnp.int32)
    tiles_rec = (jnp.arange(N_TILE * NREC, dtype=jnp.int32) // NREC).astype(jnp.int32)
    grad_total = jnp.zeros((3,) + shape, jnp.float32)
    fwd_out = []
    adj_out = []
    for shot in range(N_SHOT):
        src_idx = global_index(src_cell[shot], tiles_src)
        rec_idx = global_index(rec_cells[shot], tiles_rec)
        upper, lower, upper_old, lower_old = fwd_state[shot, 0], fwd_state[shot, 1], fwd_state[shot, 2], fwd_state[shot, 3]
        stored = []
        records = []
        for step in range(STEPS):
            horiz = second_diff(upper, 1) + second_diff(upper, 2)
            vert = second_diff(lower, 0)
            pulse = jnp.zeros((cells,), jnp.float32).at[src_idx].add(src_wave[shot, step]).reshape(shape)
            upper_next = 2.0 * upper - upper_old + speed * (stretch * horiz + couple * vert) + pulse
            lower_next = 2.0 * lower - lower_old + speed * (couple * horiz + vert) + pulse
            stored.append((horiz, vert))
            records.append(upper_next.reshape(-1)[rec_idx] - observed[shot, step])
            upper_old, lower_old, upper, lower = upper, lower, upper_next, lower_next
        fwd_out.append(jnp.stack([upper, lower]))
        lam, mu, lam_old, mu_old = adj_state[shot, 0], adj_state[shot, 1], adj_state[shot, 2], adj_state[shot, 3]
        acc_h = jnp.zeros(shape, jnp.float32)
        acc_x = jnp.zeros(shape, jnp.float32)
        acc_z = jnp.zeros(shape, jnp.float32)
        for step in reversed(range(STEPS)):
            first = speed * (stretch * lam + couple * mu)
            other = speed * (couple * lam + mu)
            inject = jnp.zeros((cells,), jnp.float32).at[rec_idx].add(records[step]).reshape(shape)
            lam_new = inject + 2.0 * lam + (second_diff(first, 1) + second_diff(first, 2)) - lam_old
            mu_new = 2.0 * mu + second_diff(other, 0) - mu_old
            horiz, vert = stored[step]
            acc_h = acc_h + lam_new * horiz
            acc_x = acc_x + lam_new * vert + mu_new * horiz
            acc_z = acc_z + mu_new * vert
            lam_old, mu_old, lam, mu = lam, mu, lam_new, mu_new
        adj_out.append(jnp.stack([lam, mu]))
        terms = jnp.stack([stretch * acc_h + couple * acc_x + acc_z, speed * acc_h, speed * acc_x])
        grad_total = grad_total + terms
    return grad_total, jnp.stack(fwd_out), jnp.stack(adj_out)
```

```python
import jax
import jax.numpy as jnp
from jax import lax
from jax.sharding import PartitionSpec as P

HALO = 12


def taps(padded, size, axis):

    def part(k):
        return lax.slice_in_dim(padded, k, k + size, axis=axis)

    return (-part(0) + 16.0 * part(1) - 30.0 * part(2) + 16.0 * part(3) - part(4)) / 12.0


def along_local(field, axis):
    pads = [(0, 0)] * field.ndim
    pads[axis] = (2, 2)
    return taps(jnp.pad(field, pads), field.shape[axis], axis)


def horiz(field):
    return along_local(field, field.ndim - 2) + along_local(field, field.ndim - 1)


def to_left_right(head, tail, axis):
    count = lax.axis_size(axis)
    from_left = lax.ppermute(tail, axis, [(i, i + 1) for i in range(count - 1)])
    from_right = lax.ppermute(head, axis, [(i + 1, i) for i in range(count - 1)])
    return from_left, from_right


def rows(x):
    return x.reshape(-1, x.shape[-1])


def per_device(coefs, fwd_state, adj_state, src_cell, src_wave, rec_cells, observed):
    w = HALO
    _, zl, ax, ay = coefs.shape
    n_tile = lax.axis_size("tile")
    tile = lax.axis_index("tile")
    steps = src_wave.shape[1]
    full = lax.all_gather(coefs, "shot", axis=1, tiled=True)
    az = full.shape[1]
    xe = ax + 2 * w
    ext_shape = (az, xe, ay)
    cells_ext = az * xe * ay

    fs = fwd_state[0]
    src_row = jnp.broadcast_to(src_cell[0, 0].astype(jnp.float32), (1, ay))
    head1 = jnp.concatenate([rows(fs[:, :, :w]), rows(coefs[:, :, :w]), src_row], axis=0)
    tail1 = jnp.concatenate([rows(fs[:, :, ax - w:]), rows(coefs[:, :, ax - w:]), src_row], axis=0)
    left1, right1 = to_left_right(head1, tail1, "tile")
    n_fs = 4 * az * w
    n_cf = 3 * zl * w

    def unpack1(m):
        st = m[:n_fs].reshape(4, az, w, ay)
        cf = m[n_fs:n_fs + n_cf].reshape(3, zl, w, ay)
        sc = m[n_fs + n_cf, 0]
        return st, cf, sc

    st_l, cf_l, sc_l = unpack1(left1)
    st_r, cf_r, sc_r = unpack1(right1)
    cf_halo = lax.all_gather(jnp.concatenate([cf_l, cf_r], axis=2), "shot", axis=1, tiled=True)
    full_ext = jnp.concatenate([cf_halo[:, :, :w], full, cf_halo[:, :, w:]], axis=2)
    speed, stretch, couple = full_ext[0], full_ext[1], full_ext[2]
    state = jnp.concatenate([st_l, fs, st_r], axis=2)

    ad = adj_state[0]
    left2, right2 = to_left_right(rows(ad[:, :, :w]), rows(ad[:, :, ax - w:]), "tile")
    adj_ext = jnp.concatenate([left2.reshape(4, az, w, ay), ad, right2.reshape(4, az, w, ay)], axis=2)

    def ext_index(cell, shift):
        depth = cell // (ax * ay)
        first = (cell // ay) % ax + shift + w
        second = cell % ay
        ok = (first >= 0) & (first < xe)
        return jnp.where(ok, (depth * xe + first) * ay + second, cells_ext), ok

    src_own, _ = ext_index(src_cell[0, 0], 0)
    src_lft, ok_l = ext_index(sc_l.astype(jnp.int32), -ax)
    src_rgt, ok_r = ext_index(sc_r.astype(jnp.int32), ax)
    ok_l = ok_l & (tile > 0)
    ok_r = ok_r & (tile < n_tile - 1)
    src_idx = jnp.stack([src_own, src_lft, src_rgt])
    src_on = jnp.stack([jnp.float32(1.0), ok_l.astype(jnp.float32), ok_r.astype(jnp.float32)])
    source_mask = jnp.zeros((cells_ext,), jnp.float32).at[src_idx].add(src_on, mode="drop").reshape(ext_shape)

    receivers = rec_cells[0]
    rec_own, _ = ext_index(receivers, 0)

    upper, lower, upper_old, lower_old = state[0], state[1], state[2], state[3]
    stored = []
    records = []
    for step in range(steps):
        h = horiz(upper)
        z = along_local(lower, 0)
        pulse = src_wave[0, step] * source_mask
        upper_next = 2.0 * upper - upper_old + speed * (stretch * h + couple * z) + pulse
        lower_next = 2.0 * lower - lower_old + speed * (couple * h + z) + pulse
        stored.append((h[:, w:w + ax], z[:, w:w + ax]))
        records.append(upper_next.reshape(-1)[rec_own] - observed[0, step])
        upper_old, lower_old, upper, lower = (upper, lower, upper_next, lower_next)

    msg = jnp.concatenate([jnp.stack(records), receivers.astype(jnp.float32)[None]], axis=0)
    left3, right3 = to_left_right(msg, msg, "tile")
    rec_l, okr_l = ext_index(left3[steps].astype(jnp.int32), -ax)
    rec_r, okr_r = ext_index(right3[steps].astype(jnp.int32), ax)
    okr_l = okr_l & (tile > 0)
    okr_r = okr_r & (tile < n_tile - 1)
    rec_l = jnp.where(okr_l, rec_l, cells_ext)
    rec_r = jnp.where(okr_r, rec_r, cells_ext)
    rec_all = jnp.concatenate([rec_own, rec_l, rec_r])

    lam, mu, lam_old, mu_old = adj_ext[0], adj_ext[1], adj_ext[2], adj_ext[3]
    acc_h = jnp.zeros((az, ax, ay), jnp.float32)
    acc_x = jnp.zeros((az, ax, ay), jnp.float32)
    acc_z = jnp.zeros((az, ax, ay), jnp.float32)
    for step in reversed(range(steps)):
        first = speed * (stretch * lam + couple * mu)
        other = speed * (couple * lam + mu)
        vals = jnp.concatenate([records[step], left3[step], right3[step]])
        inject = jnp.zeros((cells_ext,), jnp.float32).at[rec_all].add(vals, mode="drop").reshape(ext_shape)
        lam_new = inject + 2.0 * lam + horiz(first) - lam_old
        mu_new = 2.0 * mu + along_local(other, 0) - mu_old
        h, z = stored[step]
        ln = lam_new[:, w:w + ax]
        mn = mu_new[:, w:w + ax]
        acc_h = acc_h + ln * h
        acc_x = acc_x + ln * z + mn * h
        acc_z = acc_z + mn * z
        lam_old, mu_old, lam, mu = (lam, mu, lam_new, mu_new)

    n_shot = lax.axis_size("shot")
    acc = jnp.stack([acc_h, acc_x, acc_z])
    acc = acc.reshape(3, n_shot, az // n_shot, ax, ay).transpose(1, 0, 2, 3, 4)
    summed = lax.psum_scatter(acc, "shot", scatter_dimension=0, tiled=True)[0]
    q_h, q_x, q_z = summed[0], summed[1], summed[2]
    c, a, b = coefs[0], coefs[1], coefs[2]
    gradient = jnp.stack([a * q_h + b * q_x + q_z, c * q_h, c * q_x])
    fwd_final = jnp.stack([upper[:, w:w + ax], lower[:, w:w + ax]])[None]
    adj_final = jnp.stack([lam[:, w:w + ax], mu[:, w:w + ax]])[None]
    return (gradient, fwd_final, adj_final)


def solution(mesh):
    placed = (
        P(None, "shot", "tile", None),
        P("shot", None, None, "tile", None),
        P("shot", None, None, "tile", None),
        P("shot", "tile"),
        P("shot", None),
        P("shot", "tile"),
        P("shot", None, "tile"),
    )
    return jax.shard_map(
        per_device,
        mesh=mesh,
        in_specs=placed,
        out_specs=(
            P(None, "shot", "tile", None),
            P("shot", None, None, "tile", None),
            P("shot", None, None, "tile", None),
        ),
        check_vma=False,
    )
```

```python
import jax
import jax.numpy as jnp
from jax import lax
from jax.sharding import PartitionSpec as P

HALO = 12


def taps(padded, size, axis):

    def part(k):
        return lax.slice_in_dim(padded, k, k + size, axis=axis)

    return (-part(0) + 16.0 * part(1) - 30.0 * part(2) + 16.0 * part(3) - part(4)) / 12.0


def along_local(field, axis):
    pads = [(0, 0)] * field.ndim
    pads[axis] = (2, 2)
    return taps(jnp.pad(field, pads), field.shape[axis], axis)


def horiz(field):
    return along_local(field, field.ndim - 2) + along_local(field, field.ndim - 1)


def to_left_right(head, tail, axis):
    count = lax.axis_size(axis)
    from_left = lax.ppermute(tail, axis, [(i, i + 1) for i in range(count - 1)])
    from_right = lax.ppermute(head, axis, [(i + 1, i) for i in range(count - 1)])
    return from_left, from_right


def rows(x):
    return x.reshape(-1, x.shape[-1])


def per_device(coefs, fwd_state, adj_state, src_cell, src_wave, rec_cells, observed):
    w = HALO
    _, zl, ax, ay = coefs.shape
    n_tile = lax.axis_size("tile")
    tile = lax.axis_index("tile")
    steps = src_wave.shape[1]
    full = lax.all_gather(coefs, "shot", axis=1, tiled=True)
    az = full.shape[1]
    xe = ax + 2 * w
    ext_shape = (az, xe, ay)
    cells_ext = az * xe * ay

    fs = fwd_state[0]
    src_row = jnp.broadcast_to(src_cell[0, 0].astype(jnp.float32), (1, ay))
    head1 = jnp.concatenate([rows(fs[:, :, :w]), rows(coefs[:, :, :w]), src_row], axis=0)
    tail1 = jnp.concatenate([rows(fs[:, :, ax - w:]), rows(coefs[:, :, ax - w:]), src_row], axis=0)
    left1, right1 = to_left_right(head1, tail1, "tile")
    n_fs = 4 * az * w
    n_cf = 3 * zl * w

    def unpack1(m):
        st = m[:n_fs].reshape(4, az, w, ay)
        cf = m[n_fs:n_fs + n_cf].reshape(3, zl, w, ay)
        sc = m[n_fs + n_cf, 0]
        return st, cf, sc

    st_l, cf_l, sc_l = unpack1(left1)
    st_r, cf_r, sc_r = unpack1(right1)
    cf_halo = lax.all_gather(jnp.concatenate([cf_l, cf_r], axis=2), "shot", axis=1, tiled=True)
    full_ext = jnp.concatenate([cf_halo[:, :, :w], full, cf_halo[:, :, w:]], axis=2)
    speed, stretch, couple = full_ext[0], full_ext[1], full_ext[2]
    state = jnp.concatenate([st_l, fs, st_r], axis=2)


    def ext_index(cell, shift):
        depth = cell // (ax * ay)
        first = (cell // ay) % ax + shift + w
        second = cell % ay
        ok = (first >= 0) & (first < xe)
        return jnp.where(ok, (depth * xe + first) * ay + second, cells_ext), ok

    src_own, _ = ext_index(src_cell[0, 0], 0)
    src_lft, ok_l = ext_index(sc_l.astype(jnp.int32), -ax)
    src_rgt, ok_r = ext_index(sc_r.astype(jnp.int32), ax)
    ok_l = ok_l & (tile > 0)
    ok_r = ok_r & (tile < n_tile - 1)
    src_idx = jnp.stack([src_own, src_lft, src_rgt])
    src_on = jnp.stack([jnp.float32(1.0), ok_l.astype(jnp.float32), ok_r.astype(jnp.float32)])
    source_mask = jnp.zeros((cells_ext,), jnp.float32).at[src_idx].add(src_on, mode="drop").reshape(ext_shape)

    receivers = rec_cells[0]
    rec_own, _ = ext_index(receivers, 0)
    rec_row = rec_own // ay
    rec_lane = (lax.broadcasted_iota(jnp.int32, (receivers.shape[0], ay), 1) == (receivers % ay)[:, None])
    ad = adj_state[0]
    ad_head = rows(ad[:, :, :w])
    ad_tail = rows(ad[:, :, ax - w:])

    upper, lower, upper_old, lower_old = state[0], state[1], state[2], state[3]
    stored = []
    records = []
    for step in range(steps):
        h = horiz(upper)
        z = along_local(lower, 0)
        pulse = src_wave[0, step] * source_mask
        upper_next = 2.0 * upper - upper_old + speed * (stretch * h + couple * z) + pulse
        lower_next = 2.0 * lower - lower_old + speed * (couple * h + z) + pulse
        stored.append((h[:, w:w + ax], z[:, w:w + ax]))
        picked = upper_next.reshape(az * xe, ay)[rec_row]
        records.append(jnp.sum(jnp.where(rec_lane, picked, 0.0), axis=1) - observed[0, step])
        upper_old, lower_old, upper, lower = (upper, lower, upper_next, lower_next)
        if step == steps // 2 - 1:
            ad_head, ad_tail, upper = lax.optimization_barrier((ad_head, ad_tail, upper))
            left2, right2 = to_left_right(ad_head, ad_tail, "tile")
    adj_ext = jnp.concatenate([left2.reshape(4, az, w, ay), ad, right2.reshape(4, az, w, ay)], axis=2)

    msg = jnp.concatenate([jnp.stack(records), receivers.astype(jnp.float32)[None]], axis=0)
    left3, right3 = to_left_right(msg, msg, "tile")
    rec_l, okr_l = ext_index(left3[steps].astype(jnp.int32), -ax)
    rec_r, okr_r = ext_index(right3[steps].astype(jnp.int32), ax)
    okr_l = okr_l & (tile > 0)
    okr_r = okr_r & (tile < n_tile - 1)
    rec_l = jnp.where(okr_l, rec_l, cells_ext)
    rec_r = jnp.where(okr_r, rec_r, cells_ext)
    rec_all = jnp.concatenate([rec_own, rec_l, rec_r])

    lam, mu, lam_old, mu_old = adj_ext[0], adj_ext[1], adj_ext[2], adj_ext[3]
    acc_h = jnp.zeros((az, ax, ay), jnp.float32)
    acc_x = jnp.zeros((az, ax, ay), jnp.float32)
    acc_z = jnp.zeros((az, ax, ay), jnp.float32)
    for step in reversed(range(steps)):
        first = speed * (stretch * lam + couple * mu)
        other = speed * (couple * lam + mu)
        vals = jnp.concatenate([records[step], left3[step], right3[step]])
        lam_new = (2.0 * lam + horiz(first) - lam_old).reshape(-1).at[rec_all].add(vals, mode="drop").reshape(ext_shape)
        mu_new = 2.0 * mu + along_local(other, 0) - mu_old
        h, z = stored[step]
        ln = lam_new[:, w:w + ax]
        mn = mu_new[:, w:w + ax]
        acc_h = acc_h + ln * h
        acc_x = acc_x + ln * z + mn * h
        acc_z = acc_z + mn * z
        lam_old, mu_old, lam, mu = (lam, mu, lam_new, mu_new)

    n_shot = lax.axis_size("shot")
    acc = jnp.stack([acc_h, acc_x, acc_z])
    acc = acc.reshape(3, n_shot, az // n_shot, ax, ay).transpose(1, 0, 2, 3, 4)
    summed = lax.psum_scatter(acc, "shot", scatter_dimension=0, tiled=True)[0]
    q_h, q_x, q_z = summed[0], summed[1], summed[2]
    c, a, b = coefs[0], coefs[1], coefs[2]
    gradient = jnp.stack([a * q_h + b * q_x + q_z, c * q_h, c * q_x])
    fwd_final = jnp.stack([upper[:, w:w + ax], lower[:, w:w + ax]])[None]
    adj_final = jnp.stack([lam[:, w:w + ax], mu[:, w:w + ax]])[None]
    return (gradient, fwd_final, adj_final)


def solution(mesh):
    placed = (
        P(None, "shot", "tile", None),
        P("shot", None, None, "tile", None),
        P("shot", None, None, "tile", None),
        P("shot", "tile"),
        P("shot", None),
        P("shot", "tile"),
        P("shot", None, "tile"),
    )
    return jax.shard_map(
        per_device,
        mesh=mesh,
        in_specs=placed,
        out_specs=(
            P(None, "shot", "tile", None),
            P("shot", None, None, "tile", None),
            P("shot", None, None, "tile", None),
        ),
        check_vma=False,
    )
```

```python
import jax
import jax.numpy as jnp
from jax import lax
from jax.experimental import pallas as pl
from jax.experimental.pallas import tpu as pltpu
from jax.sharding import PartitionSpec as P

HALO = 12
OFF = 16
PADX = 8
INTERPRET = False


def d2(m2, m1, c0, p1, p2):
    return ((((-m2) + 16.0 * m1) - 30.0 * c0) + 16.0 * p1 - p2) * (1.0 / 12.0)


def forward_kernel(wave_ref, st_ref, cf_ref, mask_ref, h_ref, z_ref, pl_ref, q_ref, pb, qb):
    steps = h_ref.shape[0]
    az, xd, ay = st_ref.shape[1:]
    ax = h_ref.shape[2]
    pb[...] = jnp.zeros(pb.shape, jnp.float32)
    qb[...] = jnp.zeros(qb.shape, jnp.float32)
    inner = pl.ds(PADX, xd)
    pb[0, 2:2 + az, inner, :] = st_ref[0]
    qb[0, 2:2 + az, inner, :] = st_ref[1]
    pb[1, 2:2 + az, inner, :] = st_ref[2]
    qb[1, 2:2 + az, inner, :] = st_ref[3]
    lane = lax.broadcasted_iota(jnp.int32, (xd, ay), 1)
    for n in range(steps):
        cur = n % 2
        old = 1 - cur
        wv = wave_ref[n]

        def plane(d, carry):
            pc = pb[cur, d + 2, inner, :]
            d2x = d2(pb[cur, d + 2, pl.ds(PADX - 2, xd), :], pb[cur, d + 2, pl.ds(PADX - 1, xd), :], pc,
                     pb[cur, d + 2, pl.ds(PADX + 1, xd), :], pb[cur, d + 2, pl.ds(PADX + 2, xd), :])
            ym2 = jnp.where(lane >= 2, pltpu.roll(pc, 2, 1), 0.0)
            ym1 = jnp.where(lane >= 1, pltpu.roll(pc, 1, 1), 0.0)
            yp1 = jnp.where(lane < ay - 1, pltpu.roll(pc, ay - 1, 1), 0.0)
            yp2 = jnp.where(lane < ay - 2, pltpu.roll(pc, ay - 2, 1), 0.0)
            h = d2x + d2(ym2, ym1, pc, yp1, yp2)
            qc = qb[cur, d + 2, inner, :]
            z = d2(qb[cur, d, inner, :], qb[cur, d + 1, inner, :], qc, qb[cur, d + 3, inner, :], qb[cur, d + 4, inner, :])
            c = cf_ref[0, d]
            a = cf_ref[1, d]
            b = cf_ref[2, d]
            pulse = wv * mask_ref[d]
            pn = 2.0 * pc - pb[old, d + 2, inner, :] + c * (a * h + b * z) + pulse
            qn = 2.0 * qc - qb[old, d + 2, inner, :] + c * (b * h + z) + pulse
            pb[old, d + 2, inner, :] = pn
            qb[old, d + 2, inner, :] = qn
            h_ref[n, d] = h[OFF:OFF + ax]
            z_ref[n, d] = z[OFF:OFF + ax]
            pl_ref[n, d] = pn[OFF:OFF + ax]
            if n == steps - 1:
                q_ref[d] = qn[OFF:OFF + ax]
            return carry

        lax.fori_loop(0, az, plane, 0)


def run_forward(wave, st, cf, mask, ax):
    steps = wave.shape[0]
    _, az, xd, ay = st.shape
    vm = pl.BlockSpec(memory_space=pltpu.VMEM)
    loc = jax.ShapeDtypeStruct((steps, az, ax, ay), jnp.float32)
    return pl.pallas_call(
        forward_kernel,
        out_shape=(loc, loc, loc, jax.ShapeDtypeStruct((az, ax, ay), jnp.float32)),
        in_specs=[pl.BlockSpec(memory_space=pltpu.SMEM), vm, vm, vm],
        out_specs=(vm, vm, vm, vm),
        scratch_shapes=[pltpu.VMEM((2, az + 4, xd + 2 * PADX, ay), jnp.float32)] * 2,
        compiler_params=pltpu.CompilerParams(vmem_limit_bytes=60 * 1024 * 1024),
        interpret=INTERPRET,
    )(wave, st, cf, mask)


def taps(padded, size, axis):

    def part(k):
        return lax.slice_in_dim(padded, k, k + size, axis=axis)

    return (-part(0) + 16.0 * part(1) - 30.0 * part(2) + 16.0 * part(3) - part(4)) / 12.0


def along_local(field, axis):
    pads = [(0, 0)] * field.ndim
    pads[axis] = (2, 2)
    return taps(jnp.pad(field, pads), field.shape[axis], axis)


def horiz(field):
    return along_local(field, field.ndim - 2) + along_local(field, field.ndim - 1)


def to_left_right(head, tail, axis):
    count = lax.axis_size(axis)
    from_left = lax.ppermute(tail, axis, [(i, i + 1) for i in range(count - 1)])
    from_right = lax.ppermute(head, axis, [(i + 1, i) for i in range(count - 1)])
    return from_left, from_right


def rows(x):
    return x.reshape(-1, x.shape[-1])


def per_device(coefs, fwd_state, adj_state, src_cell, src_wave, rec_cells, observed):
    w = HALO
    _, zl, ax, ay = coefs.shape
    n_tile = lax.axis_size("tile")
    tile = lax.axis_index("tile")
    steps = src_wave.shape[1]
    full = lax.all_gather(coefs, "shot", axis=1, tiled=True)
    az = full.shape[1]
    xe = ax + 2 * OFF
    ext_shape = (az, xe, ay)
    cells_ext = az * xe * ay

    def widen(lo, mid, hi):
        pad = jnp.zeros(mid.shape[:-2] + (OFF - w, ay), jnp.float32)
        lo, hi = lax.optimization_barrier((jnp.concatenate([pad, lo], axis=-2), jnp.concatenate([hi, pad], axis=-2)))
        return jnp.concatenate([lo, mid, hi], axis=-2)

    fs = fwd_state[0]
    src_row = jnp.broadcast_to(src_cell[0, 0].astype(jnp.float32), (1, ay))
    head1 = jnp.concatenate([rows(fs[:, :, :w]), rows(coefs[:, :, :w]), src_row], axis=0)
    tail1 = jnp.concatenate([rows(fs[:, :, ax - w:]), rows(coefs[:, :, ax - w:]), src_row], axis=0)
    left1, right1 = to_left_right(head1, tail1, "tile")
    n_fs = 4 * az * w
    n_cf = 3 * zl * w

    def unpack1(m):
        st = m[:n_fs].reshape(4, az, w, ay)
        cf = m[n_fs:n_fs + n_cf].reshape(3, zl, w, ay)
        sc = m[n_fs + n_cf, 0]
        return st, cf, sc

    st_l, cf_l, sc_l = unpack1(left1)
    st_r, cf_r, sc_r = unpack1(right1)
    cf_halo = lax.all_gather(jnp.concatenate([cf_l, cf_r], axis=2), "shot", axis=1, tiled=True)
    full_ext = widen(cf_halo[:, :, :w], full, cf_halo[:, :, w:])
    speed, stretch, couple = full_ext[0], full_ext[1], full_ext[2]
    state = widen(st_l, fs, st_r)

    def ext_index(cell, shift):
        depth = cell // (ax * ay)
        first = (cell // ay) % ax + shift + OFF
        second = cell % ay
        ok = (first >= OFF - w) & (first < xe - OFF + w)
        return jnp.where(ok, (depth * xe + first) * ay + second, cells_ext), ok

    src_own, _ = ext_index(src_cell[0, 0], 0)
    src_lft, ok_l = ext_index(sc_l.astype(jnp.int32), -ax)
    src_rgt, ok_r = ext_index(sc_r.astype(jnp.int32), ax)
    ok_l = ok_l & (tile > 0)
    ok_r = ok_r & (tile < n_tile - 1)
    src_idx = jnp.stack([src_own, src_lft, src_rgt])
    src_on = jnp.stack([jnp.float32(1.0), ok_l.astype(jnp.float32), ok_r.astype(jnp.float32)])
    source_mask = jnp.zeros((cells_ext,), jnp.float32).at[src_idx].add(src_on, mode="drop").reshape(ext_shape)

    ad = adj_state[0]
    ad_head, ad_tail, state = lax.optimization_barrier((rows(ad[:, :, :w]), rows(ad[:, :, ax - w:]), state))
    left2, right2 = to_left_right(ad_head, ad_tail, "tile")
    adj_ext = widen(left2.reshape(4, az, w, ay), ad, right2.reshape(4, az, w, ay))

    h_all, z_all, p_all, q_last = run_forward(src_wave[0], state, full_ext, source_mask, ax)
    receivers = rec_cells[0]
    records = jnp.stack([p_all[n].reshape(-1)[receivers] for n in range(steps)]) - observed[0]

    msg = jnp.concatenate([records, receivers.astype(jnp.float32)[None]], axis=0)
    left3, right3 = to_left_right(msg, msg, "tile")
    rec_own, _ = ext_index(receivers, 0)
    rec_l, okr_l = ext_index(left3[steps].astype(jnp.int32), -ax)
    rec_r, okr_r = ext_index(right3[steps].astype(jnp.int32), ax)
    okr_l = okr_l & (tile > 0)
    okr_r = okr_r & (tile < n_tile - 1)
    rec_l = jnp.where(okr_l, rec_l, cells_ext)
    rec_r = jnp.where(okr_r, rec_r, cells_ext)
    rec_all = jnp.concatenate([rec_own, rec_l, rec_r])

    lam, mu, lam_old, mu_old = adj_ext[0], adj_ext[1], adj_ext[2], adj_ext[3]
    acc_h = jnp.zeros((az, ax, ay), jnp.float32)
    acc_x = jnp.zeros((az, ax, ay), jnp.float32)
    acc_z = jnp.zeros((az, ax, ay), jnp.float32)
    for step in reversed(range(steps)):
        first = speed * (stretch * lam + couple * mu)
        other = speed * (couple * lam + mu)
        vals = jnp.concatenate([records[step], left3[step], right3[step]])
        lam_new = (2.0 * lam + horiz(first) - lam_old).reshape(-1).at[rec_all].add(vals, mode="drop").reshape(ext_shape)
        mu_new = 2.0 * mu + along_local(other, 0) - mu_old
        h, z = h_all[step], z_all[step]
        ln = lam_new[:, OFF:OFF + ax]
        mn = mu_new[:, OFF:OFF + ax]
        acc_h = acc_h + ln * h
        acc_x = acc_x + ln * z + mn * h
        acc_z = acc_z + mn * z
        lam_old, mu_old, lam, mu = (lam, mu, lam_new, mu_new)

    n_shot = lax.axis_size("shot")
    acc = jnp.stack([acc_h, acc_x, acc_z])
    acc = acc.reshape(3, n_shot, az // n_shot, ax, ay).transpose(1, 0, 2, 3, 4)
    summed = lax.psum_scatter(acc, "shot", scatter_dimension=0, tiled=True)[0]
    q_h, q_x, q_z = summed[0], summed[1], summed[2]
    c, a, b = coefs[0], coefs[1], coefs[2]
    gradient = jnp.stack([a * q_h + b * q_x + q_z, c * q_h, c * q_x])
    fwd_final = jnp.stack([p_all[steps - 1], q_last])[None]
    adj_final = jnp.stack([lam[:, OFF:OFF + ax], mu[:, OFF:OFF + ax]])[None]
    return (gradient, fwd_final, adj_final)


def solution(mesh):
    placed = (
        P(None, "shot", "tile", None),
        P("shot", None, None, "tile", None),
        P("shot", None, None, "tile", None),
        P("shot", "tile"),
        P("shot", None),
        P("shot", "tile"),
        P("shot", None, "tile"),
    )
    return jax.shard_map(
        per_device,
        mesh=mesh,
        in_specs=placed,
        out_specs=(
            P(None, "shot", "tile", None),
            P("shot", None, None, "tile", None),
            P("shot", None, None, "tile", None),
        ),
        check_vma=False,
    )
```

```python
import jax
import jax.numpy as jnp
from jax import lax
from jax.experimental import pallas as pl
from jax.experimental.pallas import tpu as pltpu
from jax.sharding import PartitionSpec as P

HALO = 12
OFF = 16
PADX = 8
INTERPRET = False


def d2(m2, m1, c0, p1, p2):
    return ((((-m2) + 16.0 * m1) - 30.0 * c0) + 16.0 * p1 - p2) * (1.0 / 12.0)


def forward_kernel(wave_ref, st_ref, cf_ref, mask_ref, h_ref, z_ref, pl_ref, q_ref, pb, qb):
    steps = h_ref.shape[0]
    az, xd, ay = st_ref.shape[1:]
    ax = h_ref.shape[2]
    pb[...] = jnp.zeros(pb.shape, jnp.float32)
    qb[...] = jnp.zeros(qb.shape, jnp.float32)
    inner = pl.ds(PADX, xd)
    pb[0, 2:2 + az, inner, :] = st_ref[0]
    qb[0, 2:2 + az, inner, :] = st_ref[1]
    pb[1, 2:2 + az, inner, :] = st_ref[2]
    qb[1, 2:2 + az, inner, :] = st_ref[3]
    lane = lax.broadcasted_iota(jnp.int32, (xd, ay), 1)
    for n in range(steps):
        cur = n % 2
        old = 1 - cur
        wv = wave_ref[n]

        def plane(d, carry):
            pc = pb[cur, d + 2, inner, :]
            d2x = d2(pb[cur, d + 2, pl.ds(PADX - 2, xd), :], pb[cur, d + 2, pl.ds(PADX - 1, xd), :], pc,
                     pb[cur, d + 2, pl.ds(PADX + 1, xd), :], pb[cur, d + 2, pl.ds(PADX + 2, xd), :])
            ym2 = jnp.where(lane >= 2, pltpu.roll(pc, 2, 1), 0.0)
            ym1 = jnp.where(lane >= 1, pltpu.roll(pc, 1, 1), 0.0)
            yp1 = jnp.where(lane < ay - 1, pltpu.roll(pc, ay - 1, 1), 0.0)
            yp2 = jnp.where(lane < ay - 2, pltpu.roll(pc, ay - 2, 1), 0.0)
            h = d2x + d2(ym2, ym1, pc, yp1, yp2)
            qc = qb[cur, d + 2, inner, :]
            z = d2(qb[cur, d, inner, :], qb[cur, d + 1, inner, :], qc, qb[cur, d + 3, inner, :], qb[cur, d + 4, inner, :])
            c = cf_ref[0, d]
            a = cf_ref[1, d]
            b = cf_ref[2, d]
            pulse = wv * mask_ref[d]
            pn = 2.0 * pc - pb[old, d + 2, inner, :] + c * (a * h + b * z) + pulse
            qn = 2.0 * qc - qb[old, d + 2, inner, :] + c * (b * h + z) + pulse
            pb[old, d + 2, inner, :] = pn
            qb[old, d + 2, inner, :] = qn
            h_ref[n, d] = h[OFF:OFF + ax]
            z_ref[n, d] = z[OFF:OFF + ax]
            pl_ref[n, d] = pn[OFF:OFF + ax]
            if n == steps - 1:
                q_ref[d] = qn[OFF:OFF + ax]
            return carry

        lax.fori_loop(0, az, plane, 0)


def adjoint_kernel(adj_ref, cf_ref, h_ref, z_ref, e_ref, acc_ref, fin_ref, lb, mb, ob, fb):
    steps = h_ref.shape[0]
    az, xd, ay = adj_ref.shape[1:]
    ax = h_ref.shape[2]
    lb[0] = adj_ref[0]
    mb[0] = adj_ref[1]
    lb[1] = adj_ref[2]
    mb[1] = adj_ref[3]
    ob[...] = jnp.zeros(ob.shape, jnp.float32)
    fb[...] = jnp.zeros(fb.shape, jnp.float32)
    acc_ref[...] = jnp.zeros(acc_ref.shape, jnp.float32)
    lane = lax.broadcasted_iota(jnp.int32, (xd, ay), 1)
    inner = pl.ds(PADX, xd)
    for s in reversed(range(steps)):
        cur = (steps - 1 - s) % 2
        old = 1 - cur

        def other_plane(d, carry):
            ob[d + 2] = cf_ref[0, d] * (cf_ref[2, d] * lb[cur, d] + mb[cur, d])
            return carry

        lax.fori_loop(0, az, other_plane, 0)

        def plane(d, carry):
            lc = lb[cur, d]
            mc = mb[cur, d]
            c = cf_ref[0, d]
            a = cf_ref[1, d]
            b = cf_ref[2, d]
            f = c * (a * lc + b * mc)
            fb[inner, :] = f
            d2x = d2(fb[pl.ds(PADX - 2, xd), :], fb[pl.ds(PADX - 1, xd), :], f, fb[pl.ds(PADX + 1, xd), :], fb[pl.ds(PADX + 2, xd), :])
            ym2 = jnp.where(lane >= 2, pltpu.roll(f, 2, 1), 0.0)
            ym1 = jnp.where(lane >= 1, pltpu.roll(f, 1, 1), 0.0)
            yp1 = jnp.where(lane < ay - 1, pltpu.roll(f, ay - 1, 1), 0.0)
            yp2 = jnp.where(lane < ay - 2, pltpu.roll(f, ay - 2, 1), 0.0)
            hf = d2x + d2(ym2, ym1, f, yp1, yp2)
            ln = e_ref[s, d] + 2.0 * lc + hf - lb[old, d]
            mn = 2.0 * mc + d2(ob[d], ob[d + 1], ob[d + 2], ob[d + 3], ob[d + 4]) - mb[old, d]
            lb[old, d] = ln
            mb[old, d] = mn
            lo = ln[OFF:OFF + ax]
            mo = mn[OFF:OFF + ax]
            h = h_ref[s, d]
            z = z_ref[s, d]
            acc_ref[0, d] = acc_ref[0, d] + lo * h
            acc_ref[1, d] = acc_ref[1, d] + lo * z + mo * h
            acc_ref[2, d] = acc_ref[2, d] + mo * z
            if s == 0:
                fin_ref[0, d] = lo
                fin_ref[1, d] = mo
            return carry

        lax.fori_loop(0, az, plane, 0)


def run_adjoint(adj, cf, h_all, z_all, e_all):
    _, az, xd, ay = adj.shape
    ax = h_all.shape[2]
    vm = pl.BlockSpec(memory_space=pltpu.VMEM)
    return pl.pallas_call(
        adjoint_kernel,
        out_shape=(jax.ShapeDtypeStruct((3, az, ax, ay), jnp.float32), jax.ShapeDtypeStruct((2, az, ax, ay), jnp.float32)),
        in_specs=[vm] * 5,
        out_specs=(vm, vm),
        scratch_shapes=[
            pltpu.VMEM((2, az, xd, ay), jnp.float32),
            pltpu.VMEM((2, az, xd, ay), jnp.float32),
            pltpu.VMEM((az + 4, xd, ay), jnp.float32),
            pltpu.VMEM((xd + 2 * PADX, ay), jnp.float32),
        ],
        compiler_params=pltpu.CompilerParams(vmem_limit_bytes=62 * 1024 * 1024),
        interpret=INTERPRET,
    )(adj, cf, h_all, z_all, e_all)


def exact_parts(x):
    hi = x.astype(jnp.bfloat16)
    rest = x - hi.astype(jnp.float32)
    mid = rest.astype(jnp.bfloat16)
    lo = (rest - mid.astype(jnp.float32)).astype(jnp.bfloat16)
    return hi, mid, lo


def run_forward(wave, st, cf, mask, ax):
    steps = wave.shape[0]
    _, az, xd, ay = st.shape
    vm = pl.BlockSpec(memory_space=pltpu.VMEM)
    loc = jax.ShapeDtypeStruct((steps, az, ax, ay), jnp.float32)
    return pl.pallas_call(
        forward_kernel,
        out_shape=(loc, loc, loc, jax.ShapeDtypeStruct((az, ax, ay), jnp.float32)),
        in_specs=[pl.BlockSpec(memory_space=pltpu.SMEM), vm, vm, vm],
        out_specs=(vm, vm, vm, vm),
        scratch_shapes=[pltpu.VMEM((2, az + 4, xd + 2 * PADX, ay), jnp.float32)] * 2,
        compiler_params=pltpu.CompilerParams(vmem_limit_bytes=60 * 1024 * 1024),
        interpret=INTERPRET,
    )(wave, st, cf, mask)


def taps(padded, size, axis):

    def part(k):
        return lax.slice_in_dim(padded, k, k + size, axis=axis)

    return (-part(0) + 16.0 * part(1) - 30.0 * part(2) + 16.0 * part(3) - part(4)) / 12.0


def along_local(field, axis):
    pads = [(0, 0)] * field.ndim
    pads[axis] = (2, 2)
    return taps(jnp.pad(field, pads), field.shape[axis], axis)


def horiz(field):
    return along_local(field, field.ndim - 2) + along_local(field, field.ndim - 1)


def to_left_right(head, tail, axis):
    count = lax.axis_size(axis)
    from_left = lax.ppermute(tail, axis, [(i, i + 1) for i in range(count - 1)])
    from_right = lax.ppermute(head, axis, [(i + 1, i) for i in range(count - 1)])
    return from_left, from_right


def rows(x):
    return x.reshape(-1, x.shape[-1])


def per_device(coefs, fwd_state, adj_state, src_cell, src_wave, rec_cells, observed):
    w = HALO
    _, zl, ax, ay = coefs.shape
    n_tile = lax.axis_size("tile")
    tile = lax.axis_index("tile")
    steps = src_wave.shape[1]
    full = lax.all_gather(coefs, "shot", axis=1, tiled=True)
    az = full.shape[1]
    xe = ax + 2 * OFF
    ext_shape = (az, xe, ay)
    cells_ext = az * xe * ay

    def widen(lo, mid, hi):
        pad = jnp.zeros(mid.shape[:-2] + (OFF - w, ay), jnp.float32)
        lo, hi = lax.optimization_barrier((jnp.concatenate([pad, lo], axis=-2), jnp.concatenate([hi, pad], axis=-2)))
        return jnp.concatenate([lo, mid, hi], axis=-2)

    fs = fwd_state[0]
    src_row = jnp.broadcast_to(src_cell[0, 0].astype(jnp.float32), (1, ay))
    head1 = jnp.concatenate([rows(fs[:, :, :w]), rows(coefs[:, :, :w]), src_row], axis=0)
    tail1 = jnp.concatenate([rows(fs[:, :, ax - w:]), rows(coefs[:, :, ax - w:]), src_row], axis=0)
    left1, right1 = to_left_right(head1, tail1, "tile")
    n_fs = 4 * az * w
    n_cf = 3 * zl * w

    def unpack1(m):
        st = m[:n_fs].reshape(4, az, w, ay)
        cf = m[n_fs:n_fs + n_cf].reshape(3, zl, w, ay)
        sc = m[n_fs + n_cf, 0]
        return st, cf, sc

    st_l, cf_l, sc_l = unpack1(left1)
    st_r, cf_r, sc_r = unpack1(right1)
    cf_halo = lax.all_gather(jnp.concatenate([cf_l, cf_r], axis=2), "shot", axis=1, tiled=True)
    full_ext = widen(cf_halo[:, :, :w], full, cf_halo[:, :, w:])
    speed, stretch, couple = full_ext[0], full_ext[1], full_ext[2]
    state = widen(st_l, fs, st_r)

    def ext_index(cell, shift):
        depth = cell // (ax * ay)
        first = (cell // ay) % ax + shift + OFF
        second = cell % ay
        ok = (first >= OFF - w) & (first < xe - OFF + w)
        return jnp.where(ok, (depth * xe + first) * ay + second, cells_ext), ok

    src_own, _ = ext_index(src_cell[0, 0], 0)
    src_lft, ok_l = ext_index(sc_l.astype(jnp.int32), -ax)
    src_rgt, ok_r = ext_index(sc_r.astype(jnp.int32), ax)
    ok_l = ok_l & (tile > 0)
    ok_r = ok_r & (tile < n_tile - 1)
    src_idx = jnp.stack([src_own, src_lft, src_rgt])
    src_on = jnp.stack([jnp.float32(1.0), ok_l.astype(jnp.float32), ok_r.astype(jnp.float32)])
    source_mask = jnp.zeros((cells_ext,), jnp.float32).at[src_idx].add(src_on, mode="drop").reshape(ext_shape)

    ad = adj_state[0]
    ad_head, ad_tail, state = lax.optimization_barrier((rows(ad[:, :, :w]), rows(ad[:, :, ax - w:]), state))
    left2, right2 = to_left_right(ad_head, ad_tail, "tile")
    adj_ext = widen(left2.reshape(4, az, w, ay), ad, right2.reshape(4, az, w, ay))

    h_all, z_all, p_all, q_last = run_forward(src_wave[0], state, full_ext, source_mask, ax)
    receivers = rec_cells[0]
    records = jnp.stack([p_all[n].reshape(-1)[receivers] for n in range(steps)]) - observed[0]

    msg = jnp.concatenate([records, receivers.astype(jnp.float32)[None]], axis=0)
    left3, right3 = to_left_right(msg, msg, "tile")
    rec_own, _ = ext_index(receivers, 0)
    rec_l, okr_l = ext_index(left3[steps].astype(jnp.int32), -ax)
    rec_r, okr_r = ext_index(right3[steps].astype(jnp.int32), ax)
    okr_l = okr_l & (tile > 0)
    okr_r = okr_r & (tile < n_tile - 1)
    rec_l = jnp.where(okr_l, rec_l, cells_ext)
    rec_r = jnp.where(okr_r, rec_r, cells_ext)
    rec_all = jnp.concatenate([rec_own, rec_l, rec_r])

    n_rows = az * xe
    pick_row = (lax.broadcasted_iota(jnp.int32, (n_rows, rec_all.shape[0]), 0) == (rec_all // ay)[None, :]).astype(jnp.bfloat16)
    pick_lane = lax.broadcasted_iota(jnp.int32, (rec_all.shape[0], ay), 1) == (rec_all % ay)[:, None]
    dense = []
    for step in range(steps):
        vals = jnp.concatenate([records[step], left3[step], right3[step]])
        spread = jnp.where(pick_lane, vals[:, None], 0.0)
        total = None
        for part in exact_parts(spread):
            term = jnp.dot(pick_row, part, preferred_element_type=jnp.float32)
            total = term if total is None else total + term
        dense.append(total.reshape(ext_shape))
    acc, fin = run_adjoint(adj_ext, full_ext, h_all, z_all, jnp.stack(dense))
    acc_h, acc_x, acc_z = acc[0], acc[1], acc[2]

    n_shot = lax.axis_size("shot")
    acc = jnp.stack([acc_h, acc_x, acc_z])
    acc = acc.reshape(3, n_shot, az // n_shot, ax, ay).transpose(1, 0, 2, 3, 4)
    summed = lax.psum_scatter(acc, "shot", scatter_dimension=0, tiled=True)[0]
    q_h, q_x, q_z = summed[0], summed[1], summed[2]
    c, a, b = coefs[0], coefs[1], coefs[2]
    gradient = jnp.stack([a * q_h + b * q_x + q_z, c * q_h, c * q_x])
    fwd_final = jnp.stack([p_all[steps - 1], q_last])[None]
    adj_final = fin[None]
    return (gradient, fwd_final, adj_final)


def solution(mesh):
    placed = (
        P(None, "shot", "tile", None),
        P("shot", None, None, "tile", None),
        P("shot", None, None, "tile", None),
        P("shot", "tile"),
        P("shot", None),
        P("shot", "tile"),
        P("shot", None, "tile"),
    )
    return jax.shard_map(
        per_device,
        mesh=mesh,
        in_specs=placed,
        out_specs=(
            P(None, "shot", "tile", None),
            P("shot", None, None, "tile", None),
            P("shot", None, None, "tile", None),
        ),
        check_vma=False,
    )
```

```python
import jax
import jax.numpy as jnp
from jax import lax
from jax.experimental import pallas as pl
from jax.experimental.pallas import tpu as pltpu
from jax.sharding import PartitionSpec as P

HALO = 12
OFF = 16
PADX = 8
INTERPRET = False


def d2(m2, m1, c0, p1, p2):
    return ((((-m2) + 16.0 * m1) - 30.0 * c0) + 16.0 * p1 - p2) * (1.0 / 12.0)


def forward_kernel(wave_ref, st_ref, cf_ref, mask_ref, h_ref, z_ref, pl_ref, q_ref, pb, qb):
    steps = h_ref.shape[0]
    az, xd, ay = st_ref.shape[1:]
    ax = h_ref.shape[2]
    pb[...] = jnp.zeros(pb.shape, jnp.float32)
    qb[...] = jnp.zeros(qb.shape, jnp.float32)
    inner = pl.ds(PADX, xd)
    pb[0, 2:2 + az, inner, :] = st_ref[0]
    qb[0, 2:2 + az, inner, :] = st_ref[1]
    pb[1, 2:2 + az, inner, :] = st_ref[2]
    qb[1, 2:2 + az, inner, :] = st_ref[3]
    lane = lax.broadcasted_iota(jnp.int32, (xd, ay), 1)
    for n in range(steps):
        cur = n % 2
        old = 1 - cur
        wv = wave_ref[n]

        def plane(d, carry):
            pc = pb[cur, d + 2, inner, :]
            d2x = d2(pb[cur, d + 2, pl.ds(PADX - 2, xd), :], pb[cur, d + 2, pl.ds(PADX - 1, xd), :], pc,
                     pb[cur, d + 2, pl.ds(PADX + 1, xd), :], pb[cur, d + 2, pl.ds(PADX + 2, xd), :])
            ym2 = jnp.where(lane >= 2, pltpu.roll(pc, 2, 1), 0.0)
            ym1 = jnp.where(lane >= 1, pltpu.roll(pc, 1, 1), 0.0)
            yp1 = jnp.where(lane < ay - 1, pltpu.roll(pc, ay - 1, 1), 0.0)
            yp2 = jnp.where(lane < ay - 2, pltpu.roll(pc, ay - 2, 1), 0.0)
            h = d2x + d2(ym2, ym1, pc, yp1, yp2)
            qc = qb[cur, d + 2, inner, :]
            z = d2(qb[cur, d, inner, :], qb[cur, d + 1, inner, :], qc, qb[cur, d + 3, inner, :], qb[cur, d + 4, inner, :])
            c = cf_ref[0, d]
            a = cf_ref[1, d]
            b = cf_ref[2, d]
            pulse = wv * mask_ref[d]
            pn = 2.0 * pc - pb[old, d + 2, inner, :] + c * (a * h + b * z) + pulse
            qn = 2.0 * qc - qb[old, d + 2, inner, :] + c * (b * h + z) + pulse
            pb[old, d + 2, inner, :] = pn
            qb[old, d + 2, inner, :] = qn
            h_ref[n, d] = h[OFF:OFF + ax]
            z_ref[n, d] = z[OFF:OFF + ax]
            pl_ref[n, d] = pn[OFF:OFF + ax]
            if n == steps - 1:
                q_ref[d] = qn[OFF:OFF + ax]
            return carry

        lax.fori_loop(0, az, plane, 0)


def adjoint_kernel(adj_ref, cf_ref, h_ref, z_ref, row_ref, m_ref, acc_ref, fin_ref, lb, mb, ob, fb):
    steps = h_ref.shape[0]
    az, xd, ay = adj_ref.shape[1:]
    ax = h_ref.shape[2]
    lb[0] = adj_ref[0]
    mb[0] = adj_ref[1]
    lb[1] = adj_ref[2]
    mb[1] = adj_ref[3]
    ob[...] = jnp.zeros(ob.shape, jnp.float32)
    fb[...] = jnp.zeros(fb.shape, jnp.float32)
    acc_ref[...] = jnp.zeros(acc_ref.shape, jnp.float32)
    lane = lax.broadcasted_iota(jnp.int32, (xd, ay), 1)
    inner = pl.ds(PADX, xd)
    for s in reversed(range(steps)):
        cur = (steps - 1 - s) % 2
        old = 1 - cur

        def other_plane(d, carry):
            ob[d + 2] = cf_ref[0, d] * (cf_ref[2, d] * lb[cur, d] + mb[cur, d])
            return carry

        lax.fori_loop(0, az, other_plane, 0)

        def plane(d, carry):
            lc = lb[cur, d]
            mc = mb[cur, d]
            c = cf_ref[0, d]
            a = cf_ref[1, d]
            b = cf_ref[2, d]
            f = c * (a * lc + b * mc)
            fb[inner, :] = f
            d2x = d2(fb[pl.ds(PADX - 2, xd), :], fb[pl.ds(PADX - 1, xd), :], f, fb[pl.ds(PADX + 1, xd), :], fb[pl.ds(PADX + 2, xd), :])
            ym2 = jnp.where(lane >= 2, pltpu.roll(f, 2, 1), 0.0)
            ym1 = jnp.where(lane >= 1, pltpu.roll(f, 1, 1), 0.0)
            yp1 = jnp.where(lane < ay - 1, pltpu.roll(f, ay - 1, 1), 0.0)
            yp2 = jnp.where(lane < ay - 2, pltpu.roll(f, ay - 2, 1), 0.0)
            hf = d2x + d2(ym2, ym1, f, yp1, yp2)
            hit = lax.broadcasted_iota(jnp.int32, (xd, row_ref.shape[1]), 0) + d * xd == row_ref[...]
            pick = jnp.where(hit, 1.0, 0.0).astype(jnp.bfloat16)
            e = jnp.dot(pick, m_ref[s, 0], preferred_element_type=jnp.float32)
            e = e + jnp.dot(pick, m_ref[s, 1], preferred_element_type=jnp.float32)
            e = e + jnp.dot(pick, m_ref[s, 2], preferred_element_type=jnp.float32)
            ln = e + 2.0 * lc + hf - lb[old, d]
            mn = 2.0 * mc + d2(ob[d], ob[d + 1], ob[d + 2], ob[d + 3], ob[d + 4]) - mb[old, d]
            lb[old, d] = ln
            mb[old, d] = mn
            lo = ln[OFF:OFF + ax]
            mo = mn[OFF:OFF + ax]
            h = h_ref[s, d]
            z = z_ref[s, d]
            acc_ref[0, d] = acc_ref[0, d] + lo * h
            acc_ref[1, d] = acc_ref[1, d] + lo * z + mo * h
            acc_ref[2, d] = acc_ref[2, d] + mo * z
            if s == 0:
                fin_ref[0, d] = lo
                fin_ref[1, d] = mo
            return carry

        lax.fori_loop(0, az, plane, 0)


def run_adjoint(adj, cf, h_all, z_all, row, parts):
    _, az, xd, ay = adj.shape
    ax = h_all.shape[2]
    vm = pl.BlockSpec(memory_space=pltpu.VMEM)
    return pl.pallas_call(
        adjoint_kernel,
        out_shape=(jax.ShapeDtypeStruct((3, az, ax, ay), jnp.float32), jax.ShapeDtypeStruct((2, az, ax, ay), jnp.float32)),
        in_specs=[vm] * 6,
        out_specs=(vm, vm),
        scratch_shapes=[
            pltpu.VMEM((2, az, xd, ay), jnp.float32),
            pltpu.VMEM((2, az, xd, ay), jnp.float32),
            pltpu.VMEM((az + 4, xd, ay), jnp.float32),
            pltpu.VMEM((xd + 2 * PADX, ay), jnp.float32),
        ],
        compiler_params=pltpu.CompilerParams(vmem_limit_bytes=62 * 1024 * 1024),
        interpret=INTERPRET,
    )(adj, cf, h_all, z_all, row, parts)


def exact_parts(x):
    hi = lax.reduce_precision(x, exponent_bits=8, mantissa_bits=7)
    rest = x - hi
    mid = lax.reduce_precision(rest, exponent_bits=8, mantissa_bits=7)
    lo = lax.reduce_precision(rest - mid, exponent_bits=8, mantissa_bits=7)
    return hi.astype(jnp.bfloat16), mid.astype(jnp.bfloat16), lo.astype(jnp.bfloat16)


def run_forward(wave, st, cf, mask, ax):
    steps = wave.shape[0]
    _, az, xd, ay = st.shape
    vm = pl.BlockSpec(memory_space=pltpu.VMEM)
    loc = jax.ShapeDtypeStruct((steps, az, ax, ay), jnp.float32)
    return pl.pallas_call(
        forward_kernel,
        out_shape=(loc, loc, loc, jax.ShapeDtypeStruct((az, ax, ay), jnp.float32)),
        in_specs=[pl.BlockSpec(memory_space=pltpu.SMEM), vm, vm, vm],
        out_specs=(vm, vm, vm, vm),
        scratch_shapes=[pltpu.VMEM((2, az + 4, xd + 2 * PADX, ay), jnp.float32)] * 2,
        compiler_params=pltpu.CompilerParams(vmem_limit_bytes=60 * 1024 * 1024),
        interpret=INTERPRET,
    )(wave, st, cf, mask)


def taps(padded, size, axis):

    def part(k):
        return lax.slice_in_dim(padded, k, k + size, axis=axis)

    return (-part(0) + 16.0 * part(1) - 30.0 * part(2) + 16.0 * part(3) - part(4)) / 12.0


def along_local(field, axis):
    pads = [(0, 0)] * field.ndim
    pads[axis] = (2, 2)
    return taps(jnp.pad(field, pads), field.shape[axis], axis)


def horiz(field):
    return along_local(field, field.ndim - 2) + along_local(field, field.ndim - 1)


def to_left_right(head, tail, axis):
    count = lax.axis_size(axis)
    from_left = lax.ppermute(tail, axis, [(i, i + 1) for i in range(count - 1)])
    from_right = lax.ppermute(head, axis, [(i + 1, i) for i in range(count - 1)])
    return from_left, from_right


def rows(x):
    return x.reshape(-1, x.shape[-1])


def per_device(coefs, fwd_state, adj_state, src_cell, src_wave, rec_cells, observed):
    w = HALO
    _, zl, ax, ay = coefs.shape
    n_tile = lax.axis_size("tile")
    tile = lax.axis_index("tile")
    steps = src_wave.shape[1]
    full = lax.all_gather(coefs, "shot", axis=1, tiled=True)
    az = full.shape[1]
    xe = ax + 2 * OFF
    ext_shape = (az, xe, ay)
    cells_ext = az * xe * ay

    def widen(lo, mid, hi):
        pad = jnp.zeros(mid.shape[:-2] + (OFF - w, ay), jnp.float32)
        lo, hi = lax.optimization_barrier((jnp.concatenate([pad, lo], axis=-2), jnp.concatenate([hi, pad], axis=-2)))
        return jnp.concatenate([lo, mid, hi], axis=-2)

    fs = fwd_state[0]
    src_row = jnp.broadcast_to(src_cell[0, 0].astype(jnp.float32), (1, ay))
    head1 = jnp.concatenate([rows(fs[:, :, :w]), rows(coefs[:, :, :w]), src_row], axis=0)
    tail1 = jnp.concatenate([rows(fs[:, :, ax - w:]), rows(coefs[:, :, ax - w:]), src_row], axis=0)
    left1, right1 = to_left_right(head1, tail1, "tile")
    n_fs = 4 * az * w
    n_cf = 3 * zl * w

    def unpack1(m):
        st = m[:n_fs].reshape(4, az, w, ay)
        cf = m[n_fs:n_fs + n_cf].reshape(3, zl, w, ay)
        sc = m[n_fs + n_cf, 0]
        return st, cf, sc

    st_l, cf_l, sc_l = unpack1(left1)
    st_r, cf_r, sc_r = unpack1(right1)
    cf_halo = lax.all_gather(jnp.concatenate([cf_l, cf_r], axis=2), "shot", axis=1, tiled=True)
    full_ext = widen(cf_halo[:, :, :w], full, cf_halo[:, :, w:])
    speed, stretch, couple = full_ext[0], full_ext[1], full_ext[2]
    state = widen(st_l, fs, st_r)

    def ext_index(cell, shift):
        depth = cell // (ax * ay)
        first = (cell // ay) % ax + shift + OFF
        second = cell % ay
        ok = (first >= OFF - w) & (first < xe - OFF + w)
        return jnp.where(ok, (depth * xe + first) * ay + second, cells_ext), ok

    src_own, _ = ext_index(src_cell[0, 0], 0)
    src_lft, ok_l = ext_index(sc_l.astype(jnp.int32), -ax)
    src_rgt, ok_r = ext_index(sc_r.astype(jnp.int32), ax)
    ok_l = ok_l & (tile > 0)
    ok_r = ok_r & (tile < n_tile - 1)
    src_idx = jnp.stack([src_own, src_lft, src_rgt])
    src_on = jnp.stack([jnp.float32(1.0), ok_l.astype(jnp.float32), ok_r.astype(jnp.float32)])
    source_mask = jnp.zeros((cells_ext,), jnp.float32).at[src_idx].add(src_on, mode="drop").reshape(ext_shape)

    ad = adj_state[0]
    ad_head, ad_tail, state = lax.optimization_barrier((rows(ad[:, :, :w]), rows(ad[:, :, ax - w:]), state))
    left2, right2 = to_left_right(ad_head, ad_tail, "tile")
    adj_ext = widen(left2.reshape(4, az, w, ay), ad, right2.reshape(4, az, w, ay))

    h_all, z_all, p_all, q_last = run_forward(src_wave[0], state, full_ext, source_mask, ax)
    receivers = rec_cells[0]
    records = jnp.stack([p_all[n].reshape(-1)[receivers] for n in range(steps)]) - observed[0]

    msg = jnp.concatenate([records, receivers.astype(jnp.float32)[None]], axis=0)
    left3, right3 = to_left_right(msg, msg, "tile")
    rec_own, _ = ext_index(receivers, 0)
    rec_l, okr_l = ext_index(left3[steps].astype(jnp.int32), -ax)
    rec_r, okr_r = ext_index(right3[steps].astype(jnp.int32), ax)
    okr_l = okr_l & (tile > 0)
    okr_r = okr_r & (tile < n_tile - 1)
    rec_l = jnp.where(okr_l, rec_l, cells_ext)
    rec_r = jnp.where(okr_r, rec_r, cells_ext)
    rec_all = jnp.concatenate([rec_own, rec_l, rec_r])

    pick_lane = lax.broadcasted_iota(jnp.int32, (rec_all.shape[0], ay), 1) == (rec_all % ay)[:, None]
    parts = []
    for step in range(steps):
        vals = jnp.concatenate([records[step], left3[step], right3[step]])
        parts.append(jnp.stack(exact_parts(jnp.where(pick_lane, vals[:, None], 0.0))))
    rec_rows = (rec_all // ay)[None, :]
    acc, fin = run_adjoint(adj_ext, full_ext, h_all, z_all, rec_rows, jnp.stack(parts))

    n_shot = lax.axis_size("shot")
    n_y = n_shot // 2
    zc = az // n_shot
    me = lax.axis_index("shot")
    core = me % 2
    yy = me // 2
    chunks = acc.reshape(3, n_y, 2, zc, ax, ay)
    send = lax.dynamic_index_in_dim(chunks, 1 - core, axis=2, keepdims=False)
    got = lax.ppermute(send, "shot", [(i, i ^ 1) for i in range(n_shot)])
    mine = lax.dynamic_index_in_dim(chunks, core, axis=2, keepdims=False) + got
    ring = [(y * 2 + c, ((y + 1) % n_y) * 2 + c) for y in range(n_y) for c in range(2)]
    partial = lax.dynamic_index_in_dim(mine, (yy + n_y - 1) % n_y, axis=1, keepdims=False)
    for t in range(n_y - 1):
        partial = lax.ppermute(partial, "shot", ring)
        partial = partial + lax.dynamic_index_in_dim(mine, (yy + 2 * n_y - t - 2) % n_y, axis=1, keepdims=False)
    summed = partial
    q_h, q_x, q_z = summed[0], summed[1], summed[2]
    c, a, b = coefs[0], coefs[1], coefs[2]
    gradient = jnp.stack([a * q_h + b * q_x + q_z, c * q_h, c * q_x])
    fwd_final = jnp.stack([p_all[steps - 1], q_last])[None]
    adj_final = fin[None]
    return (gradient, fwd_final, adj_final)


def solution(mesh):
    placed = (
        P(None, "shot", "tile", None),
        P("shot", None, None, "tile", None),
        P("shot", None, None, "tile", None),
        P("shot", "tile"),
        P("shot", None),
        P("shot", "tile"),
        P("shot", None, "tile"),
    )
    return jax.shard_map(
        per_device,
        mesh=mesh,
        in_specs=placed,
        out_specs=(
            P(None, "shot", "tile", None),
            P("shot", None, None, "tile", None),
            P("shot", None, None, "tile", None),
        ),
        check_vma=False,
    )
```

```python
import jax
import jax.numpy as jnp
from jax import lax
from jax.experimental import pallas as pl
from jax.experimental.pallas import tpu as pltpu
from jax.sharding import PartitionSpec as P

HALO = 12
OFF = 16
PADX = 8
INTERPRET = False


def d2(m2, m1, c0, p1, p2):
    return ((((-m2) + 16.0 * m1) - 30.0 * c0) + 16.0 * p1 - p2) * (1.0 / 12.0)


def place(dst, mid, lo, hi, at):
    w = lo.shape[-2]
    ax = mid.shape[-2]
    dst[..., pl.ds(at + OFF - w, w), :] = lo
    dst[..., pl.ds(at + OFF, ax), :] = mid
    dst[..., pl.ds(at + OFF + ax, w), :] = hi


def forward_kernel(wave_ref, fs_ref, sl_ref, sr_ref, co_ref, ch_ref, mask_ref, h_ref, z_ref, pl_ref, q_ref, pb, qb, cf_ref):
    steps = h_ref.shape[0]
    az, xd, ay = mask_ref.shape
    ax = h_ref.shape[2]
    w = sl_ref.shape[2]
    pb[...] = jnp.zeros(pb.shape, jnp.float32)
    qb[...] = jnp.zeros(qb.shape, jnp.float32)
    cf_ref[...] = jnp.zeros(cf_ref.shape, jnp.float32)
    inner = pl.ds(PADX, xd)
    for k, (buf, slot) in enumerate(((pb, 0), (qb, 0), (pb, 1), (qb, 1))):
        place(buf.at[slot, 2:2 + az], fs_ref[k], sl_ref[k], sr_ref[k], PADX)
    place(cf_ref, co_ref[...], ch_ref[:, :, :w], ch_ref[:, :, w:], 0)
    lane = lax.broadcasted_iota(jnp.int32, (xd, ay), 1)
    for n in range(steps):
        cur = n % 2
        old = 1 - cur
        wv = wave_ref[n]

        def plane(d, carry):
            pc = pb[cur, d + 2, inner, :]
            d2x = d2(pb[cur, d + 2, pl.ds(PADX - 2, xd), :], pb[cur, d + 2, pl.ds(PADX - 1, xd), :], pc,
                     pb[cur, d + 2, pl.ds(PADX + 1, xd), :], pb[cur, d + 2, pl.ds(PADX + 2, xd), :])
            ym2 = jnp.where(lane >= 2, pltpu.roll(pc, 2, 1), 0.0)
            ym1 = jnp.where(lane >= 1, pltpu.roll(pc, 1, 1), 0.0)
            yp1 = jnp.where(lane < ay - 1, pltpu.roll(pc, ay - 1, 1), 0.0)
            yp2 = jnp.where(lane < ay - 2, pltpu.roll(pc, ay - 2, 1), 0.0)
            h = d2x + d2(ym2, ym1, pc, yp1, yp2)
            qc = qb[cur, d + 2, inner, :]
            z = d2(qb[cur, d, inner, :], qb[cur, d + 1, inner, :], qc, qb[cur, d + 3, inner, :], qb[cur, d + 4, inner, :])
            c = cf_ref[0, d]
            a = cf_ref[1, d]
            b = cf_ref[2, d]
            pulse = wv * mask_ref[d]
            pn = 2.0 * pc - pb[old, d + 2, inner, :] + c * (a * h + b * z) + pulse
            qn = 2.0 * qc - qb[old, d + 2, inner, :] + c * (b * h + z) + pulse
            pb[old, d + 2, inner, :] = pn
            qb[old, d + 2, inner, :] = qn
            h_ref[n, d] = h[OFF:OFF + ax]
            z_ref[n, d] = z[OFF:OFF + ax]
            pl_ref[n, d] = pn[OFF:OFF + ax]
            if n == steps - 1:
                q_ref[d] = qn[OFF:OFF + ax]
            return carry

        lax.fori_loop(0, az, plane, 0)


def adjoint_kernel(ad_ref, al_ref, ar_ref, co_ref, ch_ref, h_ref, z_ref, row_ref, m_ref, acc_ref, fin_ref, lb, mb, ob, fb, cf_ref):
    steps = h_ref.shape[0]
    az, xd, ay = ob.shape[0] - 4, ob.shape[1], ob.shape[2]
    ax = h_ref.shape[2]
    w = al_ref.shape[2]
    lb[...] = jnp.zeros(lb.shape, jnp.float32)
    mb[...] = jnp.zeros(mb.shape, jnp.float32)
    cf_ref[...] = jnp.zeros(cf_ref.shape, jnp.float32)
    for k, (buf, slot) in enumerate(((lb, 0), (mb, 0), (lb, 1), (mb, 1))):
        place(buf.at[slot], ad_ref[k], al_ref[k], ar_ref[k], 0)
    place(cf_ref, co_ref[...], ch_ref[:, :, :w], ch_ref[:, :, w:], 0)
    ob[...] = jnp.zeros(ob.shape, jnp.float32)
    fb[...] = jnp.zeros(fb.shape, jnp.float32)
    acc_ref[...] = jnp.zeros(acc_ref.shape, jnp.float32)
    lane = lax.broadcasted_iota(jnp.int32, (xd, ay), 1)
    inner = pl.ds(PADX, xd)
    for s in reversed(range(steps)):
        cur = (steps - 1 - s) % 2
        old = 1 - cur

        def other_plane(d, carry):
            ob[d + 2] = cf_ref[0, d] * (cf_ref[2, d] * lb[cur, d] + mb[cur, d])
            return carry

        lax.fori_loop(0, az, other_plane, 0)

        def plane(d, carry):
            lc = lb[cur, d]
            mc = mb[cur, d]
            c = cf_ref[0, d]
            a = cf_ref[1, d]
            b = cf_ref[2, d]
            f = c * (a * lc + b * mc)
            fb[inner, :] = f
            d2x = d2(fb[pl.ds(PADX - 2, xd), :], fb[pl.ds(PADX - 1, xd), :], f, fb[pl.ds(PADX + 1, xd), :], fb[pl.ds(PADX + 2, xd), :])
            ym2 = jnp.where(lane >= 2, pltpu.roll(f, 2, 1), 0.0)
            ym1 = jnp.where(lane >= 1, pltpu.roll(f, 1, 1), 0.0)
            yp1 = jnp.where(lane < ay - 1, pltpu.roll(f, ay - 1, 1), 0.0)
            yp2 = jnp.where(lane < ay - 2, pltpu.roll(f, ay - 2, 1), 0.0)
            hf = d2x + d2(ym2, ym1, f, yp1, yp2)
            hit = lax.broadcasted_iota(jnp.int32, (xd, row_ref.shape[1]), 0) + d * xd == row_ref[...]
            pick = jnp.where(hit, 1.0, 0.0).astype(jnp.bfloat16)
            e = jnp.dot(pick, m_ref[s, 0], preferred_element_type=jnp.float32)
            e = e + jnp.dot(pick, m_ref[s, 1], preferred_element_type=jnp.float32)
            e = e + jnp.dot(pick, m_ref[s, 2], preferred_element_type=jnp.float32)
            ln = e + 2.0 * lc + hf - lb[old, d]
            mn = 2.0 * mc + d2(ob[d], ob[d + 1], ob[d + 2], ob[d + 3], ob[d + 4]) - mb[old, d]
            lb[old, d] = ln
            mb[old, d] = mn
            lo = ln[OFF:OFF + ax]
            mo = mn[OFF:OFF + ax]
            h = h_ref[s, d]
            z = z_ref[s, d]
            acc_ref[0, d] = acc_ref[0, d] + lo * h
            acc_ref[1, d] = acc_ref[1, d] + lo * z + mo * h
            acc_ref[2, d] = acc_ref[2, d] + mo * z
            if s == 0:
                fin_ref[0, d] = lo
                fin_ref[1, d] = mo
            return carry

        lax.fori_loop(0, az, plane, 0)


def run_adjoint(ad, al, ar, co, ch, h_all, z_all, row, parts):
    _, az, ax, ay = ad.shape
    xd = ax + 2 * OFF
    vm = pl.BlockSpec(memory_space=pltpu.VMEM)
    return pl.pallas_call(
        adjoint_kernel,
        out_shape=(jax.ShapeDtypeStruct((3, az, ax, ay), jnp.float32), jax.ShapeDtypeStruct((2, az, ax, ay), jnp.float32)),
        in_specs=[vm] * 9,
        out_specs=(vm, vm),
        scratch_shapes=[
            pltpu.VMEM((2, az, xd, ay), jnp.float32),
            pltpu.VMEM((2, az, xd, ay), jnp.float32),
            pltpu.VMEM((az + 4, xd, ay), jnp.float32),
            pltpu.VMEM((xd + 2 * PADX, ay), jnp.float32),
            pltpu.VMEM((3, az, xd, ay), jnp.float32),
        ],
        compiler_params=pltpu.CompilerParams(vmem_limit_bytes=62 * 1024 * 1024),
        interpret=INTERPRET,
    )(ad, al, ar, co, ch, h_all, z_all, row, parts)


def exact_parts(x):
    hi = lax.reduce_precision(x, exponent_bits=8, mantissa_bits=7)
    rest = x - hi
    mid = lax.reduce_precision(rest, exponent_bits=8, mantissa_bits=7)
    lo = lax.reduce_precision(rest - mid, exponent_bits=8, mantissa_bits=7)
    return hi.astype(jnp.bfloat16), mid.astype(jnp.bfloat16), lo.astype(jnp.bfloat16)


def run_forward(wave, fs, sl, sr, co, ch, mask):
    steps = wave.shape[0]
    az, xd, ay = mask.shape
    ax = fs.shape[2]
    vm = pl.BlockSpec(memory_space=pltpu.VMEM)
    loc = jax.ShapeDtypeStruct((steps, az, ax, ay), jnp.float32)
    return pl.pallas_call(
        forward_kernel,
        out_shape=(loc, loc, loc, jax.ShapeDtypeStruct((az, ax, ay), jnp.float32)),
        in_specs=[pl.BlockSpec(memory_space=pltpu.SMEM)] + [vm] * 6,
        out_specs=(vm, vm, vm, vm),
        scratch_shapes=[pltpu.VMEM((2, az + 4, xd + 2 * PADX, ay), jnp.float32)] * 2 + [pltpu.VMEM((3, az, xd, ay), jnp.float32)],
        compiler_params=pltpu.CompilerParams(vmem_limit_bytes=62 * 1024 * 1024),
        interpret=INTERPRET,
    )(wave, fs, sl, sr, co, ch, mask)


def taps(padded, size, axis):

    def part(k):
        return lax.slice_in_dim(padded, k, k + size, axis=axis)

    return (-part(0) + 16.0 * part(1) - 30.0 * part(2) + 16.0 * part(3) - part(4)) / 12.0


def along_local(field, axis):
    pads = [(0, 0)] * field.ndim
    pads[axis] = (2, 2)
    return taps(jnp.pad(field, pads), field.shape[axis], axis)


def horiz(field):
    return along_local(field, field.ndim - 2) + along_local(field, field.ndim - 1)


def to_left_right(head, tail, axis):
    count = lax.axis_size(axis)
    from_left = lax.ppermute(tail, axis, [(i, i + 1) for i in range(count - 1)])
    from_right = lax.ppermute(head, axis, [(i + 1, i) for i in range(count - 1)])
    return from_left, from_right


def rows(x):
    return x.reshape(-1, x.shape[-1])


def per_device(coefs, fwd_state, adj_state, src_cell, src_wave, rec_cells, observed):
    w = HALO
    _, zl, ax, ay = coefs.shape
    n_tile = lax.axis_size("tile")
    tile = lax.axis_index("tile")
    steps = src_wave.shape[1]
    full = lax.all_gather(coefs, "shot", axis=1, tiled=True)
    az = full.shape[1]
    xe = ax + 2 * OFF
    ext_shape = (az, xe, ay)
    cells_ext = az * xe * ay

    def widen(lo, mid, hi):
        pad = jnp.zeros(mid.shape[:-2] + (OFF - w, ay), jnp.float32)
        lo, hi = lax.optimization_barrier((jnp.concatenate([pad, lo], axis=-2), jnp.concatenate([hi, pad], axis=-2)))
        return jnp.concatenate([lo, mid, hi], axis=-2)

    fs = fwd_state[0]
    src_row = jnp.broadcast_to(src_cell[0, 0].astype(jnp.float32), (1, ay))
    head1 = jnp.concatenate([rows(fs[:, :, :w]), rows(coefs[:, :, :w]), src_row], axis=0)
    tail1 = jnp.concatenate([rows(fs[:, :, ax - w:]), rows(coefs[:, :, ax - w:]), src_row], axis=0)
    left1, right1 = to_left_right(head1, tail1, "tile")
    n_fs = 4 * az * w
    n_cf = 3 * zl * w

    def unpack1(m):
        st = m[:n_fs].reshape(4, az, w, ay)
        cf = m[n_fs:n_fs + n_cf].reshape(3, zl, w, ay)
        sc = m[n_fs + n_cf, 0]
        return st, cf, sc

    st_l, cf_l, sc_l = unpack1(left1)
    st_r, cf_r, sc_r = unpack1(right1)
    cf_halo = lax.all_gather(jnp.concatenate([cf_l, cf_r], axis=2), "shot", axis=1, tiled=True)

    def ext_index(cell, shift):
        depth = cell // (ax * ay)
        first = (cell // ay) % ax + shift + OFF
        second = cell % ay
        ok = (first >= OFF - w) & (first < xe - OFF + w)
        return jnp.where(ok, (depth * xe + first) * ay + second, cells_ext), ok

    src_own, _ = ext_index(src_cell[0, 0], 0)
    src_lft, ok_l = ext_index(sc_l.astype(jnp.int32), -ax)
    src_rgt, ok_r = ext_index(sc_r.astype(jnp.int32), ax)
    ok_l = ok_l & (tile > 0)
    ok_r = ok_r & (tile < n_tile - 1)
    src_idx = jnp.stack([src_own, src_lft, src_rgt])
    src_on = jnp.stack([jnp.float32(1.0), ok_l.astype(jnp.float32), ok_r.astype(jnp.float32)])
    source_mask = jnp.zeros((cells_ext,), jnp.float32).at[src_idx].add(src_on, mode="drop").reshape(ext_shape)

    ad = adj_state[0]
    ad_head, ad_tail, st_l, st_r = lax.optimization_barrier((rows(ad[:, :, :w]), rows(ad[:, :, ax - w:]), st_l, st_r))
    left2, right2 = to_left_right(ad_head, ad_tail, "tile")

    h_all, z_all, p_all, q_last = run_forward(src_wave[0], fs, st_l, st_r, full, cf_halo, source_mask)
    receivers = rec_cells[0]
    records = jnp.stack([p_all[n].reshape(-1)[receivers] for n in range(steps)]) - observed[0]

    msg = jnp.concatenate([records, receivers.astype(jnp.float32)[None]], axis=0)
    left3, right3 = to_left_right(msg, msg, "tile")
    rec_own, _ = ext_index(receivers, 0)
    rec_l, okr_l = ext_index(left3[steps].astype(jnp.int32), -ax)
    rec_r, okr_r = ext_index(right3[steps].astype(jnp.int32), ax)
    okr_l = okr_l & (tile > 0)
    okr_r = okr_r & (tile < n_tile - 1)
    rec_l = jnp.where(okr_l, rec_l, cells_ext)
    rec_r = jnp.where(okr_r, rec_r, cells_ext)
    rec_all = jnp.concatenate([rec_own, rec_l, rec_r])

    pick_lane = lax.broadcasted_iota(jnp.int32, (rec_all.shape[0], ay), 1) == (rec_all % ay)[:, None]
    parts = []
    for step in range(steps):
        vals = jnp.concatenate([records[step], left3[step], right3[step]])
        parts.append(jnp.stack(exact_parts(jnp.where(pick_lane, vals[:, None], 0.0))))
    rec_rows = (rec_all // ay)[None, :]
    acc, fin = run_adjoint(ad, left2.reshape(4, az, w, ay), right2.reshape(4, az, w, ay), full, cf_halo, h_all, z_all, rec_rows, jnp.stack(parts))

    n_shot = lax.axis_size("shot")
    n_y = n_shot // 2
    zc = az // n_shot
    me = lax.axis_index("shot")
    core = me % 2
    yy = me // 2
    chunks = acc.reshape(3, n_y, 2, zc, ax, ay)
    send = lax.dynamic_index_in_dim(chunks, 1 - core, axis=2, keepdims=False)
    got = lax.ppermute(send, "shot", [(i, i ^ 1) for i in range(n_shot)])
    mine = lax.dynamic_index_in_dim(chunks, core, axis=2, keepdims=False) + got
    ring = [(y * 2 + c, ((y + 1) % n_y) * 2 + c) for y in range(n_y) for c in range(2)]
    partial = lax.dynamic_index_in_dim(mine, (yy + n_y - 1) % n_y, axis=1, keepdims=False)
    for t in range(n_y - 1):
        partial = lax.ppermute(partial, "shot", ring)
        partial = partial + lax.dynamic_index_in_dim(mine, (yy + 2 * n_y - t - 2) % n_y, axis=1, keepdims=False)
    summed = partial
    q_h, q_x, q_z = summed[0], summed[1], summed[2]
    c, a, b = coefs[0], coefs[1], coefs[2]
    gradient = jnp.stack([a * q_h + b * q_x + q_z, c * q_h, c * q_x])
    fwd_final = jnp.stack([p_all[steps - 1], q_last])[None]
    adj_final = fin[None]
    return (gradient, fwd_final, adj_final)


def solution(mesh):
    placed = (
        P(None, "shot", "tile", None),
        P("shot", None, None, "tile", None),
        P("shot", None, None, "tile", None),
        P("shot", "tile"),
        P("shot", None),
        P("shot", "tile"),
        P("shot", None, "tile"),
    )
    return jax.shard_map(
        per_device,
        mesh=mesh,
        in_specs=placed,
        out_specs=(
            P(None, "shot", "tile", None),
            P("shot", None, None, "tile", None),
            P("shot", None, None, "tile", None),
        ),
        check_vma=False,
    )
```

```python
import jax
import jax.numpy as jnp
from jax import lax
from jax.experimental import pallas as pl
from jax.experimental.pallas import tpu as pltpu
from jax.sharding import PartitionSpec as P

HALO = 12
OFF = 16
PADX = 8
INTERPRET = False


def d2(m2, m1, c0, p1, p2):
    return ((((-m2) + 16.0 * m1) - 30.0 * c0) + 16.0 * p1 - p2) * (1.0 / 12.0)


def place(dst, mid, lo, hi, at):
    w = lo.shape[-2]
    ax = mid.shape[-2]
    dst[..., pl.ds(at + OFF - w, w), :] = lo
    dst[..., pl.ds(at + OFF, ax), :] = mid
    dst[..., pl.ds(at + OFF + ax, w), :] = hi


def split3(x):
    hi = x.astype(jnp.bfloat16)
    rest = x - hi.astype(jnp.float32)
    mid = rest.astype(jnp.bfloat16)
    lo = (rest - mid.astype(jnp.float32)).astype(jnp.bfloat16)
    return hi, mid, lo


def forward_kernel(wave_ref, fs_ref, sl_ref, sr_ref, co_ref, ch_ref, mask_ref, rrow_ref, rlane_ref,
                   h_ref, z_ref, rec_ref, pl_ref, q_ref, pb, qb, cf_ref, racc):
    steps = h_ref.shape[0]
    az, xd, ay = mask_ref.shape
    ax = h_ref.shape[2]
    w = sl_ref.shape[2]
    pb[...] = jnp.zeros(pb.shape, jnp.float32)
    qb[...] = jnp.zeros(qb.shape, jnp.float32)
    cf_ref[...] = jnp.zeros(cf_ref.shape, jnp.float32)
    inner = pl.ds(PADX, xd)
    for k, (buf, slot) in enumerate(((pb, 0), (qb, 0), (pb, 1), (qb, 1))):
        place(buf.at[slot, 2:2 + az], fs_ref[k], sl_ref[k], sr_ref[k], PADX)
    place(cf_ref, co_ref[...], ch_ref[:, :, :w], ch_ref[:, :, w:], 0)
    lane = lax.broadcasted_iota(jnp.int32, (xd, ay), 1)
    n_rec = rrow_ref.shape[0]
    for n in range(steps):
        cur = n % 2
        old = 1 - cur
        wv = wave_ref[n]
        racc[...] = jnp.zeros(racc.shape, jnp.float32)

        def plane(d, carry):
            pc = pb[cur, d + 2, inner, :]
            d2x = d2(pb[cur, d + 2, pl.ds(PADX - 2, xd), :], pb[cur, d + 2, pl.ds(PADX - 1, xd), :], pc,
                     pb[cur, d + 2, pl.ds(PADX + 1, xd), :], pb[cur, d + 2, pl.ds(PADX + 2, xd), :])
            ym2 = jnp.where(lane >= 2, pltpu.roll(pc, 2, 1), 0.0)
            ym1 = jnp.where(lane >= 1, pltpu.roll(pc, 1, 1), 0.0)
            yp1 = jnp.where(lane < ay - 1, pltpu.roll(pc, ay - 1, 1), 0.0)
            yp2 = jnp.where(lane < ay - 2, pltpu.roll(pc, ay - 2, 1), 0.0)
            h = d2x + d2(ym2, ym1, pc, yp1, yp2)
            qc = qb[cur, d + 2, inner, :]
            z = d2(qb[cur, d, inner, :], qb[cur, d + 1, inner, :], qc, qb[cur, d + 3, inner, :], qb[cur, d + 4, inner, :])
            c = cf_ref[0, d]
            a = cf_ref[1, d]
            b = cf_ref[2, d]
            pulse = wv * mask_ref[d]
            pn = 2.0 * pc - pb[old, d + 2, inner, :] + c * (a * h + b * z) + pulse
            qn = 2.0 * qc - qb[old, d + 2, inner, :] + c * (b * h + z) + pulse
            pb[old, d + 2, inner, :] = pn
            qb[old, d + 2, inner, :] = qn
            h_ref[n, d] = h[OFF:OFF + ax]
            z_ref[n, d] = z[OFF:OFF + ax]
            po = pn[OFF:OFF + ax]
            hit = lax.broadcasted_iota(jnp.int32, (n_rec, ax), 1) + d * ax == rrow_ref[...]
            pick = jnp.where(hit, 1.0, 0.0).astype(jnp.bfloat16)
            got = None
            for part in split3(po):
                term = jnp.dot(pick, part, preferred_element_type=jnp.float32)
                got = term if got is None else got + term
            racc[...] = racc[...] + got
            if n == steps - 1:
                q_ref[d] = qn[OFF:OFF + ax]
                pl_ref[d] = po
            return carry

        lax.fori_loop(0, az, plane, 0)
        sel = lax.broadcasted_iota(jnp.int32, (n_rec, ay), 1) == rlane_ref[...]
        rec_ref[n] = jnp.where(sel, racc[...], 0.0)


def adjoint_kernel(ad_ref, al_ref, ar_ref, co_ref, ch_ref, h_ref, z_ref, row_ref, m_ref, acc_ref, fin_ref, lb, mb, ob, fb, cf_ref):
    steps = h_ref.shape[0]
    az, xd, ay = ob.shape[0] - 4, ob.shape[1], ob.shape[2]
    ax = h_ref.shape[2]
    w = al_ref.shape[2]
    lb[...] = jnp.zeros(lb.shape, jnp.float32)
    mb[...] = jnp.zeros(mb.shape, jnp.float32)
    cf_ref[...] = jnp.zeros(cf_ref.shape, jnp.float32)
    for k, (buf, slot) in enumerate(((lb, 0), (mb, 0), (lb, 1), (mb, 1))):
        place(buf.at[slot], ad_ref[k], al_ref[k], ar_ref[k], 0)
    place(cf_ref, co_ref[...], ch_ref[:, :, :w], ch_ref[:, :, w:], 0)
    ob[...] = jnp.zeros(ob.shape, jnp.float32)
    fb[...] = jnp.zeros(fb.shape, jnp.float32)
    acc_ref[...] = jnp.zeros(acc_ref.shape, jnp.float32)
    lane = lax.broadcasted_iota(jnp.int32, (xd, ay), 1)
    inner = pl.ds(PADX, xd)
    for s in reversed(range(steps)):
        cur = (steps - 1 - s) % 2
        old = 1 - cur

        def other_plane(d, carry):
            ob[d + 2] = cf_ref[0, d] * (cf_ref[2, d] * lb[cur, d] + mb[cur, d])
            return carry

        lax.fori_loop(0, az, other_plane, 0)

        def plane(d, carry):
            lc = lb[cur, d]
            mc = mb[cur, d]
            c = cf_ref[0, d]
            a = cf_ref[1, d]
            b = cf_ref[2, d]
            f = c * (a * lc + b * mc)
            fb[inner, :] = f
            d2x = d2(fb[pl.ds(PADX - 2, xd), :], fb[pl.ds(PADX - 1, xd), :], f, fb[pl.ds(PADX + 1, xd), :], fb[pl.ds(PADX + 2, xd), :])
            ym2 = jnp.where(lane >= 2, pltpu.roll(f, 2, 1), 0.0)
            ym1 = jnp.where(lane >= 1, pltpu.roll(f, 1, 1), 0.0)
            yp1 = jnp.where(lane < ay - 1, pltpu.roll(f, ay - 1, 1), 0.0)
            yp2 = jnp.where(lane < ay - 2, pltpu.roll(f, ay - 2, 1), 0.0)
            hf = d2x + d2(ym2, ym1, f, yp1, yp2)
            hit = lax.broadcasted_iota(jnp.int32, (xd, row_ref.shape[1]), 0) + d * xd == row_ref[...]
            pick = jnp.where(hit, 1.0, 0.0).astype(jnp.bfloat16)
            e = jnp.dot(pick, m_ref[s, 0], preferred_element_type=jnp.float32)
            e = e + jnp.dot(pick, m_ref[s, 1], preferred_element_type=jnp.float32)
            e = e + jnp.dot(pick, m_ref[s, 2], preferred_element_type=jnp.float32)
            ln = e + 2.0 * lc + hf - lb[old, d]
            mn = 2.0 * mc + d2(ob[d], ob[d + 1], ob[d + 2], ob[d + 3], ob[d + 4]) - mb[old, d]
            lb[old, d] = ln
            mb[old, d] = mn
            lo = ln[OFF:OFF + ax]
            mo = mn[OFF:OFF + ax]
            h = h_ref[s, d]
            z = z_ref[s, d]
            acc_ref[0, d] = acc_ref[0, d] + lo * h
            acc_ref[1, d] = acc_ref[1, d] + lo * z + mo * h
            acc_ref[2, d] = acc_ref[2, d] + mo * z
            if s == 0:
                fin_ref[0, d] = lo
                fin_ref[1, d] = mo
            return carry

        lax.fori_loop(0, az, plane, 0)


def run_adjoint(ad, al, ar, co, ch, h_all, z_all, row, parts):
    _, az, ax, ay = ad.shape
    xd = ax + 2 * OFF
    vm = pl.BlockSpec(memory_space=pltpu.VMEM)
    return pl.pallas_call(
        adjoint_kernel,
        out_shape=(jax.ShapeDtypeStruct((3, az, ax, ay), jnp.float32), jax.ShapeDtypeStruct((2, az, ax, ay), jnp.float32)),
        in_specs=[vm] * 9,
        out_specs=(vm, vm),
        scratch_shapes=[
            pltpu.VMEM((2, az, xd, ay), jnp.float32),
            pltpu.VMEM((2, az, xd, ay), jnp.float32),
            pltpu.VMEM((az + 4, xd, ay), jnp.float32),
            pltpu.VMEM((xd + 2 * PADX, ay), jnp.float32),
            pltpu.VMEM((3, az, xd, ay), jnp.float32),
        ],
        compiler_params=pltpu.CompilerParams(vmem_limit_bytes=62 * 1024 * 1024),
        interpret=INTERPRET,
    )(ad, al, ar, co, ch, h_all, z_all, row, parts)


def exact_parts(x):
    hi = lax.reduce_precision(x, exponent_bits=8, mantissa_bits=7)
    rest = x - hi
    mid = lax.reduce_precision(rest, exponent_bits=8, mantissa_bits=7)
    lo = lax.reduce_precision(rest - mid, exponent_bits=8, mantissa_bits=7)
    return hi.astype(jnp.bfloat16), mid.astype(jnp.bfloat16), lo.astype(jnp.bfloat16)


def run_forward(wave, fs, sl, sr, co, ch, mask, rrow, rlane):
    steps = wave.shape[0]
    az, xd, ay = mask.shape
    ax = fs.shape[2]
    n_rec = rrow.shape[0]
    vm = pl.BlockSpec(memory_space=pltpu.VMEM)
    loc = jax.ShapeDtypeStruct((steps, az, ax, ay), jnp.float32)
    one = jax.ShapeDtypeStruct((az, ax, ay), jnp.float32)
    return pl.pallas_call(
        forward_kernel,
        out_shape=(loc, loc, jax.ShapeDtypeStruct((steps, n_rec, ay), jnp.float32), one, one),
        in_specs=[pl.BlockSpec(memory_space=pltpu.SMEM)] + [vm] * 8,
        out_specs=(vm, vm, vm, vm, vm),
        scratch_shapes=[pltpu.VMEM((2, az + 4, xd + 2 * PADX, ay), jnp.float32)] * 2
        + [pltpu.VMEM((3, az, xd, ay), jnp.float32), pltpu.VMEM((n_rec, ay), jnp.float32)],
        compiler_params=pltpu.CompilerParams(vmem_limit_bytes=62 * 1024 * 1024),
        interpret=INTERPRET,
    )(wave, fs, sl, sr, co, ch, mask, rrow, rlane)


def taps(padded, size, axis):

    def part(k):
        return lax.slice_in_dim(padded, k, k + size, axis=axis)

    return (-part(0) + 16.0 * part(1) - 30.0 * part(2) + 16.0 * part(3) - part(4)) / 12.0


def along_local(field, axis):
    pads = [(0, 0)] * field.ndim
    pads[axis] = (2, 2)
    return taps(jnp.pad(field, pads), field.shape[axis], axis)


def horiz(field):
    return along_local(field, field.ndim - 2) + along_local(field, field.ndim - 1)


def to_left_right(head, tail, axis):
    count = lax.axis_size(axis)
    from_left = lax.ppermute(tail, axis, [(i, i + 1) for i in range(count - 1)])
    from_right = lax.ppermute(head, axis, [(i + 1, i) for i in range(count - 1)])
    return from_left, from_right


def rows(x):
    return x.reshape(-1, x.shape[-1])


def per_device(coefs, fwd_state, adj_state, src_cell, src_wave, rec_cells, observed):
    w = HALO
    _, zl, ax, ay = coefs.shape
    n_tile = lax.axis_size("tile")
    tile = lax.axis_index("tile")
    steps = src_wave.shape[1]
    full = lax.all_gather(coefs, "shot", axis=1, tiled=True)
    az = full.shape[1]
    xe = ax + 2 * OFF
    ext_shape = (az, xe, ay)
    cells_ext = az * xe * ay

    def widen(lo, mid, hi):
        pad = jnp.zeros(mid.shape[:-2] + (OFF - w, ay), jnp.float32)
        lo, hi = lax.optimization_barrier((jnp.concatenate([pad, lo], axis=-2), jnp.concatenate([hi, pad], axis=-2)))
        return jnp.concatenate([lo, mid, hi], axis=-2)

    fs = fwd_state[0]
    src_row = jnp.broadcast_to(src_cell[0, 0].astype(jnp.float32), (1, ay))
    head1 = jnp.concatenate([rows(fs[:, :, :w]), rows(coefs[:, :, :w]), src_row], axis=0)
    tail1 = jnp.concatenate([rows(fs[:, :, ax - w:]), rows(coefs[:, :, ax - w:]), src_row], axis=0)
    left1, right1 = to_left_right(head1, tail1, "tile")
    n_fs = 4 * az * w
    n_cf = 3 * zl * w

    def unpack1(m):
        st = m[:n_fs].reshape(4, az, w, ay)
        cf = m[n_fs:n_fs + n_cf].reshape(3, zl, w, ay)
        sc = m[n_fs + n_cf, 0]
        return st, cf, sc

    st_l, cf_l, sc_l = unpack1(left1)
    st_r, cf_r, sc_r = unpack1(right1)
    cf_halo = lax.all_gather(jnp.concatenate([cf_l, cf_r], axis=2), "shot", axis=1, tiled=True)

    def ext_index(cell, shift):
        depth = cell // (ax * ay)
        first = (cell // ay) % ax + shift + OFF
        second = cell % ay
        ok = (first >= OFF - w) & (first < xe - OFF + w)
        return jnp.where(ok, (depth * xe + first) * ay + second, cells_ext), ok

    src_own, _ = ext_index(src_cell[0, 0], 0)
    src_lft, ok_l = ext_index(sc_l.astype(jnp.int32), -ax)
    src_rgt, ok_r = ext_index(sc_r.astype(jnp.int32), ax)
    ok_l = ok_l & (tile > 0)
    ok_r = ok_r & (tile < n_tile - 1)
    src_idx = jnp.stack([src_own, src_lft, src_rgt])
    src_on = jnp.stack([jnp.float32(1.0), ok_l.astype(jnp.float32), ok_r.astype(jnp.float32)])
    source_mask = jnp.zeros((cells_ext,), jnp.float32).at[src_idx].add(src_on, mode="drop").reshape(ext_shape)

    ad = adj_state[0]
    ad_head, ad_tail, st_l, st_r = lax.optimization_barrier((rows(ad[:, :, :w]), rows(ad[:, :, ax - w:]), st_l, st_r))
    left2, right2 = to_left_right(ad_head, ad_tail, "tile")

    receivers = rec_cells[0]
    h_all, z_all, rec_mat, p_last, q_last = run_forward(
        src_wave[0], fs, st_l, st_r, full, cf_halo, source_mask, (receivers // ay)[:, None], (receivers % ay)[:, None])
    records = jnp.sum(rec_mat, axis=2) - observed[0]

    msg = jnp.concatenate([records, receivers.astype(jnp.float32)[None]], axis=0)
    left3, right3 = to_left_right(msg, msg, "tile")
    rec_own, _ = ext_index(receivers, 0)
    rec_l, okr_l = ext_index(left3[steps].astype(jnp.int32), -ax)
    rec_r, okr_r = ext_index(right3[steps].astype(jnp.int32), ax)
    okr_l = okr_l & (tile > 0)
    okr_r = okr_r & (tile < n_tile - 1)
    rec_l = jnp.where(okr_l, rec_l, cells_ext)
    rec_r = jnp.where(okr_r, rec_r, cells_ext)
    rec_all = jnp.concatenate([rec_own, rec_l, rec_r])

    pick_lane = lax.broadcasted_iota(jnp.int32, (rec_all.shape[0], ay), 1) == (rec_all % ay)[:, None]
    parts = []
    for step in range(steps):
        vals = jnp.concatenate([records[step], left3[step], right3[step]])
        parts.append(jnp.stack(exact_parts(jnp.where(pick_lane, vals[:, None], 0.0))))
    rec_rows = (rec_all // ay)[None, :]
    acc, fin = run_adjoint(ad, left2.reshape(4, az, w, ay), right2.reshape(4, az, w, ay), full, cf_halo, h_all, z_all, rec_rows, jnp.stack(parts))

    n_shot = lax.axis_size("shot")
    n_y = n_shot // 2
    zc = az // n_shot
    me = lax.axis_index("shot")
    core = me % 2
    yy = me // 2
    chunks = acc.reshape(3, n_y, 2, zc, ax, ay)
    send = lax.dynamic_index_in_dim(chunks, 1 - core, axis=2, keepdims=False)
    got = lax.ppermute(send, "shot", [(i, i ^ 1) for i in range(n_shot)])
    mine = lax.dynamic_index_in_dim(chunks, core, axis=2, keepdims=False) + got
    ring = [(y * 2 + c, ((y + 1) % n_y) * 2 + c) for y in range(n_y) for c in range(2)]
    partial = lax.dynamic_index_in_dim(mine, (yy + n_y - 1) % n_y, axis=1, keepdims=False)
    for t in range(n_y - 1):
        partial = lax.ppermute(partial, "shot", ring)
        partial = partial + lax.dynamic_index_in_dim(mine, (yy + 2 * n_y - t - 2) % n_y, axis=1, keepdims=False)
    summed = partial
    q_h, q_x, q_z = summed[0], summed[1], summed[2]
    c, a, b = coefs[0], coefs[1], coefs[2]
    gradient = jnp.stack([a * q_h + b * q_x + q_z, c * q_h, c * q_x])
    fwd_final = jnp.stack([p_last, q_last])[None]
    adj_final = fin[None]
    return (gradient, fwd_final, adj_final)


def solution(mesh):
    placed = (
        P(None, "shot", "tile", None),
        P("shot", None, None, "tile", None),
        P("shot", None, None, "tile", None),
        P("shot", "tile"),
        P("shot", None),
        P("shot", "tile"),
        P("shot", None, "tile"),
    )
    return jax.shard_map(
        per_device,
        mesh=mesh,
        in_specs=placed,
        out_specs=(
            P(None, "shot", "tile", None),
            P("shot", None, None, "tile", None),
            P("shot", None, None, "tile", None),
        ),
        check_vma=False,
    )
```

```python
import jax
import jax.numpy as jnp
from jax import lax
from jax.experimental import pallas as pl
from jax.experimental.pallas import tpu as pltpu
from jax.sharding import PartitionSpec as P

HALO = 12
OFF = 16
PADX = 8
INTERPRET = False


def d2(m2, m1, c0, p1, p2):
    return ((((-m2) + 16.0 * m1) - 30.0 * c0) + 16.0 * p1 - p2) * (1.0 / 12.0)


def place(dst, mid, lo, hi, at):
    w = lo.shape[-2]
    ax = mid.shape[-2]
    dst[..., pl.ds(at + OFF - w, w), :] = lo
    dst[..., pl.ds(at + OFF, ax), :] = mid
    dst[..., pl.ds(at + OFF + ax, w), :] = hi


def split3(x):
    hi = x.astype(jnp.bfloat16)
    lo = (x - hi.astype(jnp.float32)).astype(jnp.bfloat16)
    return hi, lo


def forward_kernel(wave_ref, fs_ref, sl_ref, sr_ref, co_ref, ch_ref, mask_ref, rrow_ref, rlane_ref,
                   h_ref, z_ref, rec_ref, pl_ref, q_ref, pb, qb, cf_ref, racc):
    steps = h_ref.shape[0]
    az, xd, ay = mask_ref.shape
    ax = h_ref.shape[2]
    w = sl_ref.shape[2]
    pb[...] = jnp.zeros(pb.shape, jnp.float32)
    qb[...] = jnp.zeros(qb.shape, jnp.float32)
    cf_ref[...] = jnp.zeros(cf_ref.shape, jnp.float32)
    inner = pl.ds(PADX, xd)
    for k, (buf, slot) in enumerate(((pb, 0), (qb, 0), (pb, 1), (qb, 1))):
        place(buf.at[slot, 2:2 + az], fs_ref[k], sl_ref[k], sr_ref[k], PADX)
    place(cf_ref, co_ref[...], ch_ref[:, :, :w], ch_ref[:, :, w:], 0)
    lane = lax.broadcasted_iota(jnp.int32, (xd, ay), 1)
    n_rec = rrow_ref.shape[0]
    for n in range(steps):
        cur = n % 2
        old = 1 - cur
        wv = wave_ref[n]
        racc[...] = jnp.zeros(racc.shape, jnp.float32)

        def plane(d, carry):
            pc = pb[cur, d + 2, inner, :]
            d2x = d2(pb[cur, d + 2, pl.ds(PADX - 2, xd), :], pb[cur, d + 2, pl.ds(PADX - 1, xd), :], pc,
                     pb[cur, d + 2, pl.ds(PADX + 1, xd), :], pb[cur, d + 2, pl.ds(PADX + 2, xd), :])
            ym2 = jnp.where(lane >= 2, pltpu.roll(pc, 2, 1), 0.0)
            ym1 = jnp.where(lane >= 1, pltpu.roll(pc, 1, 1), 0.0)
            yp1 = jnp.where(lane < ay - 1, pltpu.roll(pc, ay - 1, 1), 0.0)
            yp2 = jnp.where(lane < ay - 2, pltpu.roll(pc, ay - 2, 1), 0.0)
            h = d2x + d2(ym2, ym1, pc, yp1, yp2)
            qc = qb[cur, d + 2, inner, :]
            z = d2(qb[cur, d, inner, :], qb[cur, d + 1, inner, :], qc, qb[cur, d + 3, inner, :], qb[cur, d + 4, inner, :])
            c = cf_ref[0, d]
            a = cf_ref[1, d]
            b = cf_ref[2, d]
            pulse = wv * mask_ref[d]
            pn = 2.0 * pc - pb[old, d + 2, inner, :] + c * (a * h + b * z) + pulse
            qn = 2.0 * qc - qb[old, d + 2, inner, :] + c * (b * h + z) + pulse
            pb[old, d + 2, inner, :] = pn
            qb[old, d + 2, inner, :] = qn
            h_ref[n, d] = h[OFF:OFF + ax]
            z_ref[n, d] = z[OFF:OFF + ax]
            po = pn[OFF:OFF + ax]
            hit = lax.broadcasted_iota(jnp.int32, (n_rec, ax), 1) + d * ax == rrow_ref[...]
            pick = jnp.where(hit, 1.0, 0.0).astype(jnp.bfloat16)
            got = None
            for part in split3(po):
                term = jnp.dot(pick, part, preferred_element_type=jnp.float32)
                got = term if got is None else got + term
            racc[...] = racc[...] + got
            if n == steps - 1:
                q_ref[d] = qn[OFF:OFF + ax]
                pl_ref[d] = po
            return carry

        lax.fori_loop(0, az, plane, 0)
        sel = lax.broadcasted_iota(jnp.int32, (n_rec, ay), 1) == rlane_ref[...]
        rec_ref[n] = jnp.where(sel, racc[...], 0.0)


def adjoint_kernel(ad_ref, al_ref, ar_ref, co_ref, ch_ref, h_ref, z_ref, row_ref, m_ref, acc_ref, fin_ref, lb, mb, ob, fb, cf_ref):
    steps = h_ref.shape[0]
    az, xd, ay = ob.shape[0] - 4, ob.shape[1], ob.shape[2]
    ax = h_ref.shape[2]
    w = al_ref.shape[2]
    lb[...] = jnp.zeros(lb.shape, jnp.float32)
    mb[...] = jnp.zeros(mb.shape, jnp.float32)
    cf_ref[...] = jnp.zeros(cf_ref.shape, jnp.float32)
    for k, (buf, slot) in enumerate(((lb, 0), (mb, 0), (lb, 1), (mb, 1))):
        place(buf.at[slot], ad_ref[k], al_ref[k], ar_ref[k], 0)
    place(cf_ref, co_ref[...], ch_ref[:, :, :w], ch_ref[:, :, w:], 0)
    ob[...] = jnp.zeros(ob.shape, jnp.float32)
    fb[...] = jnp.zeros(fb.shape, jnp.float32)
    acc_ref[...] = jnp.zeros(acc_ref.shape, jnp.float32)
    lane = lax.broadcasted_iota(jnp.int32, (xd, ay), 1)
    inner = pl.ds(PADX, xd)
    for s in reversed(range(steps)):
        cur = (steps - 1 - s) % 2
        old = 1 - cur

        def other_plane(d, carry):
            ob[d + 2] = cf_ref[0, d] * (cf_ref[2, d] * lb[cur, d] + mb[cur, d])
            return carry

        lax.fori_loop(0, az, other_plane, 0)

        def plane(d, carry):
            lc = lb[cur, d]
            mc = mb[cur, d]
            c = cf_ref[0, d]
            a = cf_ref[1, d]
            b = cf_ref[2, d]
            f = c * (a * lc + b * mc)
            fb[inner, :] = f
            d2x = d2(fb[pl.ds(PADX - 2, xd), :], fb[pl.ds(PADX - 1, xd), :], f, fb[pl.ds(PADX + 1, xd), :], fb[pl.ds(PADX + 2, xd), :])
            ym2 = jnp.where(lane >= 2, pltpu.roll(f, 2, 1), 0.0)
            ym1 = jnp.where(lane >= 1, pltpu.roll(f, 1, 1), 0.0)
            yp1 = jnp.where(lane < ay - 1, pltpu.roll(f, ay - 1, 1), 0.0)
            yp2 = jnp.where(lane < ay - 2, pltpu.roll(f, ay - 2, 1), 0.0)
            hf = d2x + d2(ym2, ym1, f, yp1, yp2)
            hit = lax.broadcasted_iota(jnp.int32, (xd, row_ref.shape[1]), 0) + d * xd == row_ref[...]
            pick = jnp.where(hit, 1.0, 0.0).astype(jnp.bfloat16)
            e = jnp.dot(pick, m_ref[s, 0], preferred_element_type=jnp.float32)
            e = e + jnp.dot(pick, m_ref[s, 1], preferred_element_type=jnp.float32)
            ln = e + 2.0 * lc + hf - lb[old, d]
            mn = 2.0 * mc + d2(ob[d], ob[d + 1], ob[d + 2], ob[d + 3], ob[d + 4]) - mb[old, d]
            lb[old, d] = ln
            mb[old, d] = mn
            lo = ln[OFF:OFF + ax]
            mo = mn[OFF:OFF + ax]
            h = h_ref[s, d]
            z = z_ref[s, d]
            acc_ref[0, d] = acc_ref[0, d] + lo * h
            acc_ref[1, d] = acc_ref[1, d] + lo * z + mo * h
            acc_ref[2, d] = acc_ref[2, d] + mo * z
            if s == 0:
                fin_ref[0, d] = lo
                fin_ref[1, d] = mo
            return carry

        lax.fori_loop(0, az, plane, 0)


def run_adjoint(ad, al, ar, co, ch, h_all, z_all, row, parts):
    _, az, ax, ay = ad.shape
    xd = ax + 2 * OFF
    vm = pl.BlockSpec(memory_space=pltpu.VMEM)
    return pl.pallas_call(
        adjoint_kernel,
        out_shape=(jax.ShapeDtypeStruct((3, az, ax, ay), jnp.float32), jax.ShapeDtypeStruct((2, az, ax, ay), jnp.float32)),
        in_specs=[vm] * 9,
        out_specs=(vm, vm),
        scratch_shapes=[
            pltpu.VMEM((2, az, xd, ay), jnp.float32),
            pltpu.VMEM((2, az, xd, ay), jnp.float32),
            pltpu.VMEM((az + 4, xd, ay), jnp.float32),
            pltpu.VMEM((xd + 2 * PADX, ay), jnp.float32),
            pltpu.VMEM((3, az, xd, ay), jnp.float32),
        ],
        compiler_params=pltpu.CompilerParams(vmem_limit_bytes=62 * 1024 * 1024),
        interpret=INTERPRET,
    )(ad, al, ar, co, ch, h_all, z_all, row, parts)


def exact_parts(x):
    hi = lax.reduce_precision(x, exponent_bits=8, mantissa_bits=7)
    rest = x - hi
    lo = lax.reduce_precision(rest, exponent_bits=8, mantissa_bits=7)
    return hi.astype(jnp.bfloat16), lo.astype(jnp.bfloat16)


def run_forward(wave, fs, sl, sr, co, ch, mask, rrow, rlane):
    steps = wave.shape[0]
    az, xd, ay = mask.shape
    ax = fs.shape[2]
    n_rec = rrow.shape[0]
    vm = pl.BlockSpec(memory_space=pltpu.VMEM)
    loc = jax.ShapeDtypeStruct((steps, az, ax, ay), jnp.float32)
    one = jax.ShapeDtypeStruct((az, ax, ay), jnp.float32)
    return pl.pallas_call(
        forward_kernel,
        out_shape=(loc, loc, jax.ShapeDtypeStruct((steps, n_rec, ay), jnp.float32), one, one),
        in_specs=[pl.BlockSpec(memory_space=pltpu.SMEM)] + [vm] * 8,
        out_specs=(vm, vm, vm, vm, vm),
        scratch_shapes=[pltpu.VMEM((2, az + 4, xd + 2 * PADX, ay), jnp.float32)] * 2
        + [pltpu.VMEM((3, az, xd, ay), jnp.float32), pltpu.VMEM((n_rec, ay), jnp.float32)],
        compiler_params=pltpu.CompilerParams(vmem_limit_bytes=62 * 1024 * 1024),
        interpret=INTERPRET,
    )(wave, fs, sl, sr, co, ch, mask, rrow, rlane)


def taps(padded, size, axis):

    def part(k):
        return lax.slice_in_dim(padded, k, k + size, axis=axis)

    return (-part(0) + 16.0 * part(1) - 30.0 * part(2) + 16.0 * part(3) - part(4)) / 12.0


def along_local(field, axis):
    pads = [(0, 0)] * field.ndim
    pads[axis] = (2, 2)
    return taps(jnp.pad(field, pads), field.shape[axis], axis)


def horiz(field):
    return along_local(field, field.ndim - 2) + along_local(field, field.ndim - 1)


def to_left_right(head, tail, axis):
    count = lax.axis_size(axis)
    from_left = lax.ppermute(tail, axis, [(i, i + 1) for i in range(count - 1)])
    from_right = lax.ppermute(head, axis, [(i + 1, i) for i in range(count - 1)])
    return from_left, from_right


def rows(x):
    return x.reshape(-1, x.shape[-1])


def per_device(coefs, fwd_state, adj_state, src_cell, src_wave, rec_cells, observed):
    w = HALO
    _, zl, ax, ay = coefs.shape
    n_tile = lax.axis_size("tile")
    tile = lax.axis_index("tile")
    steps = src_wave.shape[1]
    full = lax.all_gather(coefs, "shot", axis=1, tiled=True)
    az = full.shape[1]
    xe = ax + 2 * OFF
    ext_shape = (az, xe, ay)
    cells_ext = az * xe * ay

    def widen(lo, mid, hi):
        pad = jnp.zeros(mid.shape[:-2] + (OFF - w, ay), jnp.float32)
        lo, hi = lax.optimization_barrier((jnp.concatenate([pad, lo], axis=-2), jnp.concatenate([hi, pad], axis=-2)))
        return jnp.concatenate([lo, mid, hi], axis=-2)

    fs = fwd_state[0]
    src_row = jnp.broadcast_to(src_cell[0, 0].astype(jnp.float32), (1, ay))
    head1 = jnp.concatenate([rows(fs[:, :, :w]), rows(coefs[:, :, :w]), src_row], axis=0)
    tail1 = jnp.concatenate([rows(fs[:, :, ax - w:]), rows(coefs[:, :, ax - w:]), src_row], axis=0)
    left1, right1 = to_left_right(head1, tail1, "tile")
    n_fs = 4 * az * w
    n_cf = 3 * zl * w

    def unpack1(m):
        st = m[:n_fs].reshape(4, az, w, ay)
        cf = m[n_fs:n_fs + n_cf].reshape(3, zl, w, ay)
        sc = m[n_fs + n_cf, 0]
        return st, cf, sc

    st_l, cf_l, sc_l = unpack1(left1)
    st_r, cf_r, sc_r = unpack1(right1)
    cf_halo = lax.all_gather(jnp.concatenate([cf_l, cf_r], axis=2), "shot", axis=1, tiled=True)

    def ext_index(cell, shift):
        depth = cell // (ax * ay)
        first = (cell // ay) % ax + shift + OFF
        second = cell % ay
        ok = (first >= OFF - w) & (first < xe - OFF + w)
        return jnp.where(ok, (depth * xe + first) * ay + second, cells_ext), ok

    src_own, _ = ext_index(src_cell[0, 0], 0)
    src_lft, ok_l = ext_index(sc_l.astype(jnp.int32), -ax)
    src_rgt, ok_r = ext_index(sc_r.astype(jnp.int32), ax)
    ok_l = ok_l & (tile > 0)
    ok_r = ok_r & (tile < n_tile - 1)
    src_idx = jnp.stack([src_own, src_lft, src_rgt])
    src_on = jnp.stack([jnp.float32(1.0), ok_l.astype(jnp.float32), ok_r.astype(jnp.float32)])
    source_mask = jnp.zeros((cells_ext,), jnp.float32).at[src_idx].add(src_on, mode="drop").reshape(ext_shape)

    ad = adj_state[0]
    ad_head, ad_tail, st_l, st_r = lax.optimization_barrier((rows(ad[:, :, :w]), rows(ad[:, :, ax - w:]), st_l, st_r))
    left2, right2 = to_left_right(ad_head, ad_tail, "tile")

    receivers = rec_cells[0]
    h_all, z_all, rec_mat, p_last, q_last = run_forward(
        src_wave[0], fs, st_l, st_r, full, cf_halo, source_mask, (receivers // ay)[:, None], (receivers % ay)[:, None])
    records = jnp.sum(rec_mat, axis=2) - observed[0]

    msg = jnp.concatenate([records, receivers.astype(jnp.float32)[None]], axis=0)
    left3, right3 = to_left_right(msg, msg, "tile")
    rec_own, _ = ext_index(receivers, 0)
    rec_l, okr_l = ext_index(left3[steps].astype(jnp.int32), -ax)
    rec_r, okr_r = ext_index(right3[steps].astype(jnp.int32), ax)
    okr_l = okr_l & (tile > 0)
    okr_r = okr_r & (tile < n_tile - 1)
    rec_l = jnp.where(okr_l, rec_l, cells_ext)
    rec_r = jnp.where(okr_r, rec_r, cells_ext)
    rec_all = jnp.concatenate([rec_own, rec_l, rec_r])

    pick_lane = lax.broadcasted_iota(jnp.int32, (rec_all.shape[0], ay), 1) == (rec_all % ay)[:, None]
    parts = []
    for step in range(steps):
        vals = jnp.concatenate([records[step], left3[step], right3[step]])
        parts.append(jnp.stack(exact_parts(jnp.where(pick_lane, vals[:, None], 0.0))))
    rec_rows = (rec_all // ay)[None, :]
    acc, fin = run_adjoint(ad, left2.reshape(4, az, w, ay), right2.reshape(4, az, w, ay), full, cf_halo, h_all, z_all, rec_rows, jnp.stack(parts))

    n_shot = lax.axis_size("shot")
    n_y = n_shot // 2
    zc = az // n_shot
    me = lax.axis_index("shot")
    core = me % 2
    yy = me // 2
    chunks = acc.reshape(3, n_y, 2, zc, ax, ay)
    send = lax.dynamic_index_in_dim(chunks, 1 - core, axis=2, keepdims=False)
    got = lax.ppermute(send, "shot", [(i, i ^ 1) for i in range(n_shot)])
    mine = lax.dynamic_index_in_dim(chunks, core, axis=2, keepdims=False) + got
    ring = [(y * 2 + c, ((y + 1) % n_y) * 2 + c) for y in range(n_y) for c in range(2)]
    partial = lax.dynamic_index_in_dim(mine, (yy + n_y - 1) % n_y, axis=1, keepdims=False)
    for t in range(n_y - 1):
        partial = lax.ppermute(partial, "shot", ring)
        partial = partial + lax.dynamic_index_in_dim(mine, (yy + 2 * n_y - t - 2) % n_y, axis=1, keepdims=False)
    summed = partial
    q_h, q_x, q_z = summed[0], summed[1], summed[2]
    c, a, b = coefs[0], coefs[1], coefs[2]
    gradient = jnp.stack([a * q_h + b * q_x + q_z, c * q_h, c * q_x])
    fwd_final = jnp.stack([p_last, q_last])[None]
    adj_final = fin[None]
    return (gradient, fwd_final, adj_final)


def solution(mesh):
    placed = (
        P(None, "shot", "tile", None),
        P("shot", None, None, "tile", None),
        P("shot", None, None, "tile", None),
        P("shot", "tile"),
        P("shot", None),
        P("shot", "tile"),
        P("shot", None, "tile"),
    )
    return jax.shard_map(
        per_device,
        mesh=mesh,
        in_specs=placed,
        out_specs=(
            P(None, "shot", "tile", None),
            P("shot", None, None, "tile", None),
            P("shot", None, None, "tile", None),
        ),
        check_vma=False,
    )
```

```python
import jax
import jax.numpy as jnp
from jax import lax
from jax.experimental import pallas as pl
from jax.experimental.pallas import tpu as pltpu
from jax.sharding import PartitionSpec as P

HALO = 12
OFF = 16
PADX = 8
INTERPRET = False


def d2(m2, m1, c0, p1, p2):
    return ((((-m2) + 16.0 * m1) - 30.0 * c0) + 16.0 * p1 - p2) * (1.0 / 12.0)


def place(dst, mid, lo, hi, at):
    w = lo.shape[-2]
    ax = mid.shape[-2]
    dst[..., pl.ds(at + OFF - w, w), :] = lo
    dst[..., pl.ds(at + OFF, ax), :] = mid
    dst[..., pl.ds(at + OFF + ax, w), :] = hi


def split3(x):
    hi = x.astype(jnp.bfloat16)
    lo = (x - hi.astype(jnp.float32)).astype(jnp.bfloat16)
    return hi, lo


def forward_kernel(wave_ref, fs_ref, sl_ref, sr_ref, co_ref, ch_ref, mask_ref, rrow_ref, rlane_ref,
                   h_ref, z_ref, rec_ref, pl_ref, q_ref, pb, qb, cf_ref, plocal, pickf):
    steps = h_ref.shape[0]
    az, xd, ay = mask_ref.shape
    ax = h_ref.shape[2]
    w = sl_ref.shape[2]
    pb[...] = jnp.zeros(pb.shape, jnp.float32)
    qb[...] = jnp.zeros(qb.shape, jnp.float32)
    cf_ref[...] = jnp.zeros(cf_ref.shape, jnp.float32)
    inner = pl.ds(PADX, xd)
    for k, (buf, slot) in enumerate(((pb, 0), (qb, 0), (pb, 1), (qb, 1))):
        place(buf.at[slot, 2:2 + az], fs_ref[k], sl_ref[k], sr_ref[k], PADX)
    place(cf_ref, co_ref[...], ch_ref[:, :, :w], ch_ref[:, :, w:], 0)
    lane = lax.broadcasted_iota(jnp.int32, (xd, ay), 1)
    n_rec = rrow_ref.shape[0]
    pickf[...] = jnp.where(lax.broadcasted_iota(jnp.int32, pickf.shape, 1) == rrow_ref[...], 1.0, 0.0).astype(jnp.bfloat16)
    for n in range(steps):
        cur = n % 2
        old = 1 - cur
        wv = wave_ref[n]

        def plane(d, carry):
            pc = pb[cur, d + 2, inner, :]
            d2x = d2(pb[cur, d + 2, pl.ds(PADX - 2, xd), :], pb[cur, d + 2, pl.ds(PADX - 1, xd), :], pc,
                     pb[cur, d + 2, pl.ds(PADX + 1, xd), :], pb[cur, d + 2, pl.ds(PADX + 2, xd), :])
            ym2 = jnp.where(lane >= 2, pltpu.roll(pc, 2, 1), 0.0)
            ym1 = jnp.where(lane >= 1, pltpu.roll(pc, 1, 1), 0.0)
            yp1 = jnp.where(lane < ay - 1, pltpu.roll(pc, ay - 1, 1), 0.0)
            yp2 = jnp.where(lane < ay - 2, pltpu.roll(pc, ay - 2, 1), 0.0)
            h = d2x + d2(ym2, ym1, pc, yp1, yp2)
            qc = qb[cur, d + 2, inner, :]
            z = d2(qb[cur, d, inner, :], qb[cur, d + 1, inner, :], qc, qb[cur, d + 3, inner, :], qb[cur, d + 4, inner, :])
            c = cf_ref[0, d]
            a = cf_ref[1, d]
            b = cf_ref[2, d]
            pulse = wv * mask_ref[d]
            pn = 2.0 * pc - pb[old, d + 2, inner, :] + c * (a * h + b * z) + pulse
            qn = 2.0 * qc - qb[old, d + 2, inner, :] + c * (b * h + z) + pulse
            pb[old, d + 2, inner, :] = pn
            qb[old, d + 2, inner, :] = qn
            h_ref[n, d] = h[OFF:OFF + ax]
            z_ref[n, d] = z[OFF:OFF + ax]
            po = pn[OFF:OFF + ax]
            plocal[pl.ds(pl.multiple_of(d * ax, ax), ax), :] = po
            if n == steps - 1:
                q_ref[d] = qn[OFF:OFF + ax]
                pl_ref[d] = po
            return carry

        lax.fori_loop(0, az, plane, 0)
        got = None
        for part in split3(plocal[...]):
            term = jnp.dot(pickf[...], part, preferred_element_type=jnp.float32)
            got = term if got is None else got + term
        sel = lax.broadcasted_iota(jnp.int32, (n_rec, ay), 1) == rlane_ref[...]
        rec_ref[n] = jnp.where(sel, got, 0.0)


def adjoint_kernel(ad_ref, al_ref, ar_ref, co_ref, ch_ref, h_ref, z_ref, row_ref, m_ref, acc_ref, fin_ref, lb, mb, ob, fb, cf_ref,
                   picka, eb):
    steps = h_ref.shape[0]
    az, xd, ay = ob.shape[0] - 4, ob.shape[1], ob.shape[2]
    ax = h_ref.shape[2]
    w = al_ref.shape[2]
    lb[...] = jnp.zeros(lb.shape, jnp.float32)
    mb[...] = jnp.zeros(mb.shape, jnp.float32)
    cf_ref[...] = jnp.zeros(cf_ref.shape, jnp.float32)
    for k, (buf, slot) in enumerate(((lb, 0), (mb, 0), (lb, 1), (mb, 1))):
        place(buf.at[slot], ad_ref[k], al_ref[k], ar_ref[k], 0)
    place(cf_ref, co_ref[...], ch_ref[:, :, :w], ch_ref[:, :, w:], 0)
    picka[...] = jnp.where(lax.broadcasted_iota(jnp.int32, picka.shape, 0) == row_ref[...], 1.0, 0.0).astype(jnp.bfloat16)
    ob[...] = jnp.zeros(ob.shape, jnp.float32)
    fb[...] = jnp.zeros(fb.shape, jnp.float32)
    acc_ref[...] = jnp.zeros(acc_ref.shape, jnp.float32)
    lane = lax.broadcasted_iota(jnp.int32, (xd, ay), 1)
    inner = pl.ds(PADX, xd)
    for s in reversed(range(steps)):
        cur = (steps - 1 - s) % 2
        old = 1 - cur

        def other_plane(d, carry):
            ob[d + 2] = cf_ref[0, d] * (cf_ref[2, d] * lb[cur, d] + mb[cur, d])
            return carry

        lax.fori_loop(0, az, other_plane, 0)
        eb[...] = (jnp.dot(picka[...], m_ref[s, 0], preferred_element_type=jnp.float32)
                   + jnp.dot(picka[...], m_ref[s, 1], preferred_element_type=jnp.float32))

        def plane(d, carry):
            lc = lb[cur, d]
            mc = mb[cur, d]
            c = cf_ref[0, d]
            a = cf_ref[1, d]
            b = cf_ref[2, d]
            f = c * (a * lc + b * mc)
            fb[inner, :] = f
            d2x = d2(fb[pl.ds(PADX - 2, xd), :], fb[pl.ds(PADX - 1, xd), :], f, fb[pl.ds(PADX + 1, xd), :], fb[pl.ds(PADX + 2, xd), :])
            ym2 = jnp.where(lane >= 2, pltpu.roll(f, 2, 1), 0.0)
            ym1 = jnp.where(lane >= 1, pltpu.roll(f, 1, 1), 0.0)
            yp1 = jnp.where(lane < ay - 1, pltpu.roll(f, ay - 1, 1), 0.0)
            yp2 = jnp.where(lane < ay - 2, pltpu.roll(f, ay - 2, 1), 0.0)
            hf = d2x + d2(ym2, ym1, f, yp1, yp2)
            e = eb[pl.ds(pl.multiple_of(d * xd, 8), xd), :]
            ln = e + 2.0 * lc + hf - lb[old, d]
            mn = 2.0 * mc + d2(ob[d], ob[d + 1], ob[d + 2], ob[d + 3], ob[d + 4]) - mb[old, d]
            lb[old, d] = ln
            mb[old, d] = mn
            lo = ln[OFF:OFF + ax]
            mo = mn[OFF:OFF + ax]
            h = h_ref[s, d]
            z = z_ref[s, d]
            acc_ref[0, d] = acc_ref[0, d] + lo * h
            acc_ref[1, d] = acc_ref[1, d] + lo * z + mo * h
            acc_ref[2, d] = acc_ref[2, d] + mo * z
            if s == 0:
                fin_ref[0, d] = lo
                fin_ref[1, d] = mo
            return carry

        lax.fori_loop(0, az, plane, 0)


def run_adjoint(ad, al, ar, co, ch, h_all, z_all, row, parts):
    _, az, ax, ay = ad.shape
    xd = ax + 2 * OFF
    vm = pl.BlockSpec(memory_space=pltpu.VMEM)
    return pl.pallas_call(
        adjoint_kernel,
        out_shape=(jax.ShapeDtypeStruct((3, az, ax, ay), jnp.float32), jax.ShapeDtypeStruct((2, az, ax, ay), jnp.float32)),
        in_specs=[vm] * 9,
        out_specs=(vm, vm),
        scratch_shapes=[
            pltpu.VMEM((2, az, xd, ay), jnp.float32),
            pltpu.VMEM((2, az, xd, ay), jnp.float32),
            pltpu.VMEM((az + 4, xd, ay), jnp.float32),
            pltpu.VMEM((xd + 2 * PADX, ay), jnp.float32),
            pltpu.VMEM((3, az, xd, ay), jnp.float32),
            pltpu.VMEM((az * xd, row.shape[1]), jnp.bfloat16),
            pltpu.VMEM((az * xd, ay), jnp.float32),
        ],
        compiler_params=pltpu.CompilerParams(vmem_limit_bytes=62 * 1024 * 1024),
        interpret=INTERPRET,
    )(ad, al, ar, co, ch, h_all, z_all, row, parts)


def exact_parts(x):
    hi = lax.reduce_precision(x, exponent_bits=8, mantissa_bits=7)
    rest = x - hi
    lo = lax.reduce_precision(rest, exponent_bits=8, mantissa_bits=7)
    return hi.astype(jnp.bfloat16), lo.astype(jnp.bfloat16)


def run_forward(wave, fs, sl, sr, co, ch, mask, rrow, rlane):
    steps = wave.shape[0]
    az, xd, ay = mask.shape
    ax = fs.shape[2]
    n_rec = rrow.shape[0]
    vm = pl.BlockSpec(memory_space=pltpu.VMEM)
    loc = jax.ShapeDtypeStruct((steps, az, ax, ay), jnp.float32)
    one = jax.ShapeDtypeStruct((az, ax, ay), jnp.float32)
    return pl.pallas_call(
        forward_kernel,
        out_shape=(loc, loc, jax.ShapeDtypeStruct((steps, n_rec, ay), jnp.float32), one, one),
        in_specs=[pl.BlockSpec(memory_space=pltpu.SMEM)] + [vm] * 8,
        out_specs=(vm, vm, vm, vm, vm),
        scratch_shapes=[pltpu.VMEM((2, az + 4, xd + 2 * PADX, ay), jnp.float32)] * 2
        + [pltpu.VMEM((3, az, xd, ay), jnp.float32), pltpu.VMEM((az * ax, ay), jnp.float32),
           pltpu.VMEM((n_rec, az * ax), jnp.bfloat16)],
        compiler_params=pltpu.CompilerParams(vmem_limit_bytes=62 * 1024 * 1024),
        interpret=INTERPRET,
    )(wave, fs, sl, sr, co, ch, mask, rrow, rlane)


def taps(padded, size, axis):

    def part(k):
        return lax.slice_in_dim(padded, k, k + size, axis=axis)

    return (-part(0) + 16.0 * part(1) - 30.0 * part(2) + 16.0 * part(3) - part(4)) / 12.0


def along_local(field, axis):
    pads = [(0, 0)] * field.ndim
    pads[axis] = (2, 2)
    return taps(jnp.pad(field, pads), field.shape[axis], axis)


def horiz(field):
    return along_local(field, field.ndim - 2) + along_local(field, field.ndim - 1)


def to_left_right(head, tail, axis):
    count = lax.axis_size(axis)
    from_left = lax.ppermute(tail, axis, [(i, i + 1) for i in range(count - 1)])
    from_right = lax.ppermute(head, axis, [(i + 1, i) for i in range(count - 1)])
    return from_left, from_right


def rows(x):
    return x.reshape(-1, x.shape[-1])


def per_device(coefs, fwd_state, adj_state, src_cell, src_wave, rec_cells, observed):
    w = HALO
    _, zl, ax, ay = coefs.shape
    n_tile = lax.axis_size("tile")
    tile = lax.axis_index("tile")
    steps = src_wave.shape[1]
    full = lax.all_gather(coefs, "shot", axis=1, tiled=True)
    az = full.shape[1]
    xe = ax + 2 * OFF
    ext_shape = (az, xe, ay)
    cells_ext = az * xe * ay

    def widen(lo, mid, hi):
        pad = jnp.zeros(mid.shape[:-2] + (OFF - w, ay), jnp.float32)
        lo, hi = lax.optimization_barrier((jnp.concatenate([pad, lo], axis=-2), jnp.concatenate([hi, pad], axis=-2)))
        return jnp.concatenate([lo, mid, hi], axis=-2)

    fs = fwd_state[0]
    src_row = jnp.broadcast_to(src_cell[0, 0].astype(jnp.float32), (1, ay))
    head1 = jnp.concatenate([rows(fs[:, :, :w]), rows(coefs[:, :, :w]), src_row], axis=0)
    tail1 = jnp.concatenate([rows(fs[:, :, ax - w:]), rows(coefs[:, :, ax - w:]), src_row], axis=0)
    left1, right1 = to_left_right(head1, tail1, "tile")
    n_fs = 4 * az * w
    n_cf = 3 * zl * w

    def unpack1(m):
        st = m[:n_fs].reshape(4, az, w, ay)
        cf = m[n_fs:n_fs + n_cf].reshape(3, zl, w, ay)
        sc = m[n_fs + n_cf, 0]
        return st, cf, sc

    st_l, cf_l, sc_l = unpack1(left1)
    st_r, cf_r, sc_r = unpack1(right1)
    cf_halo = lax.all_gather(jnp.concatenate([cf_l, cf_r], axis=2), "shot", axis=1, tiled=True)

    def ext_index(cell, shift):
        depth = cell // (ax * ay)
        first = (cell // ay) % ax + shift + OFF
        second = cell % ay
        ok = (first >= OFF - w) & (first < xe - OFF + w)
        return jnp.where(ok, (depth * xe + first) * ay + second, cells_ext), ok

    src_own, _ = ext_index(src_cell[0, 0], 0)
    src_lft, ok_l = ext_index(sc_l.astype(jnp.int32), -ax)
    src_rgt, ok_r = ext_index(sc_r.astype(jnp.int32), ax)
    ok_l = ok_l & (tile > 0)
    ok_r = ok_r & (tile < n_tile - 1)
    src_idx = jnp.stack([src_own, src_lft, src_rgt])
    src_on = jnp.stack([jnp.float32(1.0), ok_l.astype(jnp.float32), ok_r.astype(jnp.float32)])
    source_mask = jnp.zeros((cells_ext,), jnp.float32).at[src_idx].add(src_on, mode="drop").reshape(ext_shape)

    ad = adj_state[0]
    ad_head, ad_tail, st_l, st_r = lax.optimization_barrier((rows(ad[:, :, :w]), rows(ad[:, :, ax - w:]), st_l, st_r))
    left2, right2 = to_left_right(ad_head, ad_tail, "tile")

    receivers = rec_cells[0]
    h_all, z_all, rec_mat, p_last, q_last = run_forward(
        src_wave[0], fs, st_l, st_r, full, cf_halo, source_mask, (receivers // ay)[:, None], (receivers % ay)[:, None])
    records = jnp.sum(rec_mat, axis=2) - observed[0]

    msg = jnp.concatenate([records, receivers.astype(jnp.float32)[None]], axis=0)
    left3, right3 = to_left_right(msg, msg, "tile")
    rec_own, _ = ext_index(receivers, 0)
    rec_l, okr_l = ext_index(left3[steps].astype(jnp.int32), -ax)
    rec_r, okr_r = ext_index(right3[steps].astype(jnp.int32), ax)
    okr_l = okr_l & (tile > 0)
    okr_r = okr_r & (tile < n_tile - 1)
    rec_l = jnp.where(okr_l, rec_l, cells_ext)
    rec_r = jnp.where(okr_r, rec_r, cells_ext)
    rec_all = jnp.concatenate([rec_own, rec_l, rec_r])

    pick_lane = lax.broadcasted_iota(jnp.int32, (rec_all.shape[0], ay), 1) == (rec_all % ay)[:, None]
    parts = []
    for step in range(steps):
        vals = jnp.concatenate([records[step], left3[step], right3[step]])
        parts.append(jnp.stack(exact_parts(jnp.where(pick_lane, vals[:, None], 0.0))))
    rec_rows = (rec_all // ay)[None, :]
    acc, fin = run_adjoint(ad, left2.reshape(4, az, w, ay), right2.reshape(4, az, w, ay), full, cf_halo, h_all, z_all, rec_rows, jnp.stack(parts))

    n_shot = lax.axis_size("shot")
    n_y = n_shot // 2
    zc = az // n_shot
    me = lax.axis_index("shot")
    core = me % 2
    yy = me // 2
    chunks = acc.reshape(3, n_y, 2, zc, ax, ay)
    send = lax.dynamic_index_in_dim(chunks, 1 - core, axis=2, keepdims=False)
    got = lax.ppermute(send, "shot", [(i, i ^ 1) for i in range(n_shot)])
    mine = lax.dynamic_index_in_dim(chunks, core, axis=2, keepdims=False) + got
    ring = [(y * 2 + c, ((y + 1) % n_y) * 2 + c) for y in range(n_y) for c in range(2)]
    partial = lax.dynamic_index_in_dim(mine, (yy + n_y - 1) % n_y, axis=1, keepdims=False)
    for t in range(n_y - 1):
        partial = lax.ppermute(partial, "shot", ring)
        partial = partial + lax.dynamic_index_in_dim(mine, (yy + 2 * n_y - t - 2) % n_y, axis=1, keepdims=False)
    summed = partial
    q_h, q_x, q_z = summed[0], summed[1], summed[2]
    c, a, b = coefs[0], coefs[1], coefs[2]
    gradient = jnp.stack([a * q_h + b * q_x + q_z, c * q_h, c * q_x])
    fwd_final = jnp.stack([p_last, q_last])[None]
    adj_final = fin[None]
    return (gradient, fwd_final, adj_final)


def solution(mesh):
    placed = (
        P(None, "shot", "tile", None),
        P("shot", None, None, "tile", None),
        P("shot", None, None, "tile", None),
        P("shot", "tile"),
        P("shot", None),
        P("shot", "tile"),
        P("shot", None, "tile"),
    )
    return jax.shard_map(
        per_device,
        mesh=mesh,
        in_specs=placed,
        out_specs=(
            P(None, "shot", "tile", None),
            P("shot", None, None, "tile", None),
            P("shot", None, None, "tile", None),
        ),
        check_vma=False,
    )
```

```python
import jax
import jax.numpy as jnp
from jax import lax
from jax.experimental import pallas as pl
from jax.experimental.pallas import tpu as pltpu
from jax.sharding import PartitionSpec as P

HALO = 12
OFF = 16
PADX = 8
INTERPRET = False


def d2(m2, m1, c0, p1, p2):
    return ((((-m2) + 16.0 * m1) - 30.0 * c0) + 16.0 * p1 - p2) * (1.0 / 12.0)


def place(dst, mid, lo, hi, at):
    w = lo.shape[-2]
    ax = mid.shape[-2]
    dst[..., pl.ds(at + OFF - w, w), :] = lo
    dst[..., pl.ds(at + OFF, ax), :] = mid
    dst[..., pl.ds(at + OFF + ax, w), :] = hi


def split3(x):
    hi = x.astype(jnp.bfloat16)
    lo = (x - hi.astype(jnp.float32)).astype(jnp.bfloat16)
    return hi, lo


def forward_kernel(wave_ref, fs_ref, sl_ref, sr_ref, co_ref, ch_ref, mask_ref, rrow_ref, rlane_ref,
                   h_ref, z_ref, rec_ref, pl_ref, q_ref, pb, qb, cf_ref, plocal, pickf):
    steps = h_ref.shape[0]
    az, xd, ay = mask_ref.shape
    ax = h_ref.shape[2]
    w = sl_ref.shape[2]
    pb[...] = jnp.zeros(pb.shape, jnp.float32)
    qb[...] = jnp.zeros(qb.shape, jnp.float32)
    cf_ref[...] = jnp.zeros(cf_ref.shape, jnp.float32)
    inner = pl.ds(PADX, xd)
    for k, (buf, slot) in enumerate(((pb, 0), (qb, 0), (pb, 1), (qb, 1))):
        place(buf.at[slot, 2:2 + az], fs_ref[k], sl_ref[k], sr_ref[k], PADX)
    place(cf_ref, co_ref[...], ch_ref[:, :, :w], ch_ref[:, :, w:], 0)
    lane = lax.broadcasted_iota(jnp.int32, (xd, ay), 1)
    n_rec = rrow_ref.shape[0]
    pickf[...] = jnp.where(lax.broadcasted_iota(jnp.int32, pickf.shape, 1) == rrow_ref[...], 1.0, 0.0).astype(jnp.bfloat16)
    for n in range(steps):
        cur = n % 2
        old = 1 - cur
        wv = wave_ref[n]

        def plane(d, carry):
            pc = pb[cur, d + 2, inner, :]
            d2x = d2(pb[cur, d + 2, pl.ds(PADX - 2, xd), :], pb[cur, d + 2, pl.ds(PADX - 1, xd), :], pc,
                     pb[cur, d + 2, pl.ds(PADX + 1, xd), :], pb[cur, d + 2, pl.ds(PADX + 2, xd), :])
            ym2 = jnp.where(lane >= 2, pltpu.roll(pc, 2, 1), 0.0)
            ym1 = jnp.where(lane >= 1, pltpu.roll(pc, 1, 1), 0.0)
            yp1 = jnp.where(lane < ay - 1, pltpu.roll(pc, ay - 1, 1), 0.0)
            yp2 = jnp.where(lane < ay - 2, pltpu.roll(pc, ay - 2, 1), 0.0)
            h = d2x + d2(ym2, ym1, pc, yp1, yp2)
            qc = qb[cur, d + 2, inner, :]
            z = d2(qb[cur, d, inner, :], qb[cur, d + 1, inner, :], qc, qb[cur, d + 3, inner, :], qb[cur, d + 4, inner, :])
            c = cf_ref[0, d]
            a = cf_ref[1, d]
            b = cf_ref[2, d]
            pulse = wv * mask_ref[d]
            pn = 2.0 * pc - pb[old, d + 2, inner, :] + c * (a * h + b * z) + pulse
            qn = 2.0 * qc - qb[old, d + 2, inner, :] + c * (b * h + z) + pulse
            pb[old, d + 2, inner, :] = pn
            qb[old, d + 2, inner, :] = qn
            h_ref[n, d] = h[OFF:OFF + ax]
            z_ref[n, d] = z[OFF:OFF + ax]
            po = pn[OFF:OFF + ax]
            plocal[pl.ds(pl.multiple_of(d * ax, ax), ax), :] = po
            if n == steps - 1:
                q_ref[d] = qn[OFF:OFF + ax]
                pl_ref[d] = po
            return carry

        lax.fori_loop(0, az, plane, 0)
        got = None
        for part in split3(plocal[...]):
            term = jnp.dot(pickf[...], part, preferred_element_type=jnp.float32)
            got = term if got is None else got + term
        sel = lax.broadcasted_iota(jnp.int32, (n_rec, ay), 1) == rlane_ref[...]
        rec_ref[n] = jnp.where(sel, got, 0.0)


def adjoint_kernel(ad_ref, al_ref, ar_ref, co_ref, ch_ref, h_ref, z_ref, row_ref, m_ref, acc_ref, fin_ref, lb, mb, ob, fb, cf_ref):
    steps = h_ref.shape[0]
    az, xd, ay = ob.shape[0] - 4, ob.shape[1], ob.shape[2]
    ax = h_ref.shape[2]
    w = al_ref.shape[2]
    lb[...] = jnp.zeros(lb.shape, jnp.float32)
    mb[...] = jnp.zeros(mb.shape, jnp.float32)
    cf_ref[...] = jnp.zeros(cf_ref.shape, jnp.float32)
    for k, (buf, slot) in enumerate(((lb, 0), (mb, 0), (lb, 1), (mb, 1))):
        place(buf.at[slot], ad_ref[k], al_ref[k], ar_ref[k], 0)
    place(cf_ref, co_ref[...], ch_ref[:, :, :w], ch_ref[:, :, w:], 0)
    ob[...] = jnp.zeros(ob.shape, jnp.float32)
    fb[...] = jnp.zeros(fb.shape, jnp.float32)
    acc_ref[...] = jnp.zeros(acc_ref.shape, jnp.float32)
    lane = lax.broadcasted_iota(jnp.int32, (xd, ay), 1)
    inner = pl.ds(PADX, xd)
    for s in reversed(range(steps)):
        cur = (steps - 1 - s) % 2
        old = 1 - cur

        def other_plane(d, carry):
            ob[d + 2] = cf_ref[0, d] * (cf_ref[2, d] * lb[cur, d] + mb[cur, d])
            return carry

        lax.fori_loop(0, az, other_plane, 0)

        def plane(d, carry):
            lc = lb[cur, d]
            mc = mb[cur, d]
            c = cf_ref[0, d]
            a = cf_ref[1, d]
            b = cf_ref[2, d]
            f = c * (a * lc + b * mc)
            fb[inner, :] = f
            d2x = d2(fb[pl.ds(PADX - 2, xd), :], fb[pl.ds(PADX - 1, xd), :], f, fb[pl.ds(PADX + 1, xd), :], fb[pl.ds(PADX + 2, xd), :])
            ym2 = jnp.where(lane >= 2, pltpu.roll(f, 2, 1), 0.0)
            ym1 = jnp.where(lane >= 1, pltpu.roll(f, 1, 1), 0.0)
            yp1 = jnp.where(lane < ay - 1, pltpu.roll(f, ay - 1, 1), 0.0)
            yp2 = jnp.where(lane < ay - 2, pltpu.roll(f, ay - 2, 1), 0.0)
            hf = d2x + d2(ym2, ym1, f, yp1, yp2)
            hit = lax.broadcasted_iota(jnp.int32, (xd, row_ref.shape[1]), 0) + d * xd == row_ref[...]
            pick = jnp.where(hit, 1.0, 0.0).astype(jnp.bfloat16)
            e = jnp.dot(pick, m_ref[s, 0], preferred_element_type=jnp.float32)
            e = e + jnp.dot(pick, m_ref[s, 1], preferred_element_type=jnp.float32)
            ln = e + 2.0 * lc + hf - lb[old, d]
            mn = 2.0 * mc + d2(ob[d], ob[d + 1], ob[d + 2], ob[d + 3], ob[d + 4]) - mb[old, d]
            lb[old, d] = ln
            mb[old, d] = mn
            lo = ln[OFF:OFF + ax]
            mo = mn[OFF:OFF + ax]
            h = h_ref[s, d]
            z = z_ref[s, d]
            acc_ref[0, d] = acc_ref[0, d] + lo * h
            acc_ref[1, d] = acc_ref[1, d] + lo * z + mo * h
            acc_ref[2, d] = acc_ref[2, d] + mo * z
            if s == 0:
                fin_ref[0, d] = lo
                fin_ref[1, d] = mo
            return carry

        lax.fori_loop(0, az, plane, 0)


def run_adjoint(ad, al, ar, co, ch, h_all, z_all, row, parts):
    _, az, ax, ay = ad.shape
    xd = ax + 2 * OFF
    vm = pl.BlockSpec(memory_space=pltpu.VMEM)
    return pl.pallas_call(
        adjoint_kernel,
        out_shape=(jax.ShapeDtypeStruct((3, az, ax, ay), jnp.float32), jax.ShapeDtypeStruct((2, az, ax, ay), jnp.float32)),
        in_specs=[vm] * 9,
        out_specs=(vm, vm),
        scratch_shapes=[
            pltpu.VMEM((2, az, xd, ay), jnp.float32),
            pltpu.VMEM((2, az, xd, ay), jnp.float32),
            pltpu.VMEM((az + 4, xd, ay), jnp.float32),
            pltpu.VMEM((xd + 2 * PADX, ay), jnp.float32),
            pltpu.VMEM((3, az, xd, ay), jnp.float32),
        ],
        compiler_params=pltpu.CompilerParams(vmem_limit_bytes=62 * 1024 * 1024),
        interpret=INTERPRET,
    )(ad, al, ar, co, ch, h_all, z_all, row, parts)


def exact_parts(x):
    hi = lax.reduce_precision(x, exponent_bits=8, mantissa_bits=7)
    rest = x - hi
    lo = lax.reduce_precision(rest, exponent_bits=8, mantissa_bits=7)
    return hi.astype(jnp.bfloat16), lo.astype(jnp.bfloat16)


def run_forward(wave, fs, sl, sr, co, ch, mask, rrow, rlane):
    steps = wave.shape[0]
    az, xd, ay = mask.shape
    ax = fs.shape[2]
    n_rec = rrow.shape[0]
    vm = pl.BlockSpec(memory_space=pltpu.VMEM)
    loc = jax.ShapeDtypeStruct((steps, az, ax, ay), jnp.float32)
    one = jax.ShapeDtypeStruct((az, ax, ay), jnp.float32)
    return pl.pallas_call(
        forward_kernel,
        out_shape=(loc, loc, jax.ShapeDtypeStruct((steps, n_rec, ay), jnp.float32), one, one),
        in_specs=[pl.BlockSpec(memory_space=pltpu.SMEM)] + [vm] * 8,
        out_specs=(vm, vm, vm, vm, vm),
        scratch_shapes=[pltpu.VMEM((2, az + 4, xd + 2 * PADX, ay), jnp.float32)] * 2
        + [pltpu.VMEM((3, az, xd, ay), jnp.float32), pltpu.VMEM((az * ax, ay), jnp.float32),
           pltpu.VMEM((n_rec, az * ax), jnp.bfloat16)],
        compiler_params=pltpu.CompilerParams(vmem_limit_bytes=62 * 1024 * 1024),
        interpret=INTERPRET,
    )(wave, fs, sl, sr, co, ch, mask, rrow, rlane)


def taps(padded, size, axis):

    def part(k):
        return lax.slice_in_dim(padded, k, k + size, axis=axis)

    return (-part(0) + 16.0 * part(1) - 30.0 * part(2) + 16.0 * part(3) - part(4)) / 12.0


def along_local(field, axis):
    pads = [(0, 0)] * field.ndim
    pads[axis] = (2, 2)
    return taps(jnp.pad(field, pads), field.shape[axis], axis)


def horiz(field):
    return along_local(field, field.ndim - 2) + along_local(field, field.ndim - 1)


def to_left_right(head, tail, axis):
    count = lax.axis_size(axis)
    from_left = lax.ppermute(tail, axis, [(i, i + 1) for i in range(count - 1)])
    from_right = lax.ppermute(head, axis, [(i + 1, i) for i in range(count - 1)])
    return from_left, from_right


def rows(x):
    return x.reshape(-1, x.shape[-1])


def per_device(coefs, fwd_state, adj_state, src_cell, src_wave, rec_cells, observed):
    w = HALO
    _, zl, ax, ay = coefs.shape
    n_tile = lax.axis_size("tile")
    tile = lax.axis_index("tile")
    steps = src_wave.shape[1]
    full = lax.all_gather(coefs, "shot", axis=1, tiled=True)
    az = full.shape[1]
    xe = ax + 2 * OFF
    ext_shape = (az, xe, ay)
    cells_ext = az * xe * ay

    def widen(lo, mid, hi):
        pad = jnp.zeros(mid.shape[:-2] + (OFF - w, ay), jnp.float32)
        lo, hi = lax.optimization_barrier((jnp.concatenate([pad, lo], axis=-2), jnp.concatenate([hi, pad], axis=-2)))
        return jnp.concatenate([lo, mid, hi], axis=-2)

    fs = fwd_state[0]
    src_row = jnp.broadcast_to(src_cell[0, 0].astype(jnp.float32), (1, ay))
    head1 = jnp.concatenate([rows(fs[:, :, :w]), rows(coefs[:, :, :w]), src_row], axis=0)
    tail1 = jnp.concatenate([rows(fs[:, :, ax - w:]), rows(coefs[:, :, ax - w:]), src_row], axis=0)
    left1, right1 = to_left_right(head1, tail1, "tile")
    n_fs = 4 * az * w
    n_cf = 3 * zl * w

    def unpack1(m):
        st = m[:n_fs].reshape(4, az, w, ay)
        cf = m[n_fs:n_fs + n_cf].reshape(3, zl, w, ay)
        sc = m[n_fs + n_cf, 0]
        return st, cf, sc

    st_l, cf_l, sc_l = unpack1(left1)
    st_r, cf_r, sc_r = unpack1(right1)
    cf_halo = lax.all_gather(jnp.concatenate([cf_l, cf_r], axis=2), "shot", axis=1, tiled=True)

    def ext_index(cell, shift):
        depth = cell // (ax * ay)
        first = (cell // ay) % ax + shift + OFF
        second = cell % ay
        ok = (first >= OFF - w) & (first < xe - OFF + w)
        return jnp.where(ok, (depth * xe + first) * ay + second, cells_ext), ok

    src_own, _ = ext_index(src_cell[0, 0], 0)
    src_lft, ok_l = ext_index(sc_l.astype(jnp.int32), -ax)
    src_rgt, ok_r = ext_index(sc_r.astype(jnp.int32), ax)
    ok_l = ok_l & (tile > 0)
    ok_r = ok_r & (tile < n_tile - 1)
    src_idx = jnp.stack([src_own, src_lft, src_rgt])
    src_on = jnp.stack([jnp.float32(1.0), ok_l.astype(jnp.float32), ok_r.astype(jnp.float32)])
    source_mask = jnp.zeros((cells_ext,), jnp.float32).at[src_idx].add(src_on, mode="drop").reshape(ext_shape)

    ad = adj_state[0]
    ad_head, ad_tail, st_l, st_r = lax.optimization_barrier((rows(ad[:, :, :w]), rows(ad[:, :, ax - w:]), st_l, st_r))
    left2, right2 = to_left_right(ad_head, ad_tail, "tile")

    receivers = rec_cells[0]
    h_all, z_all, rec_mat, p_last, q_last = run_forward(
        src_wave[0], fs, st_l, st_r, full, cf_halo, source_mask, (receivers // ay)[:, None], (receivers % ay)[:, None])
    records = jnp.sum(rec_mat, axis=2) - observed[0]

    msg = jnp.concatenate([records, receivers.astype(jnp.float32)[None]], axis=0)
    left3, right3 = to_left_right(msg, msg, "tile")
    rec_own, _ = ext_index(receivers, 0)
    rec_l, okr_l = ext_index(left3[steps].astype(jnp.int32), -ax)
    rec_r, okr_r = ext_index(right3[steps].astype(jnp.int32), ax)
    okr_l = okr_l & (tile > 0)
    okr_r = okr_r & (tile < n_tile - 1)
    rec_l = jnp.where(okr_l, rec_l, cells_ext)
    rec_r = jnp.where(okr_r, rec_r, cells_ext)
    rec_all = jnp.concatenate([rec_own, rec_l, rec_r])

    pick_lane = lax.broadcasted_iota(jnp.int32, (rec_all.shape[0], ay), 1) == (rec_all % ay)[:, None]
    parts = []
    for step in range(steps):
        vals = jnp.concatenate([records[step], left3[step], right3[step]])
        parts.append(jnp.stack(exact_parts(jnp.where(pick_lane, vals[:, None], 0.0))))
    rec_rows = (rec_all // ay)[None, :]
    acc, fin = run_adjoint(ad, left2.reshape(4, az, w, ay), right2.reshape(4, az, w, ay), full, cf_halo, h_all, z_all, rec_rows, jnp.stack(parts))

    n_shot = lax.axis_size("shot")
    n_y = n_shot // 2
    zc = az // n_shot
    me = lax.axis_index("shot")
    core = me % 2
    yy = me // 2
    chunks = acc.reshape(3, n_y, 2, zc, ax, ay)
    send = lax.dynamic_index_in_dim(chunks, 1 - core, axis=2, keepdims=False)
    got = lax.ppermute(send, "shot", [(i, i ^ 1) for i in range(n_shot)])
    mine = lax.dynamic_index_in_dim(chunks, core, axis=2, keepdims=False) + got
    ring = [(y * 2 + c, ((y + 1) % n_y) * 2 + c) for y in range(n_y) for c in range(2)]
    partial = lax.dynamic_index_in_dim(mine, (yy + n_y - 1) % n_y, axis=1, keepdims=False)
    for t in range(n_y - 1):
        partial = lax.ppermute(partial, "shot", ring)
        partial = partial + lax.dynamic_index_in_dim(mine, (yy + 2 * n_y - t - 2) % n_y, axis=1, keepdims=False)
    summed = partial
    q_h, q_x, q_z = summed[0], summed[1], summed[2]
    c, a, b = coefs[0], coefs[1], coefs[2]
    gradient = jnp.stack([a * q_h + b * q_x + q_z, c * q_h, c * q_x])
    fwd_final = jnp.stack([p_last, q_last])[None]
    adj_final = fin[None]
    return (gradient, fwd_final, adj_final)


def solution(mesh):
    placed = (
        P(None, "shot", "tile", None),
        P("shot", None, None, "tile", None),
        P("shot", None, None, "tile", None),
        P("shot", "tile"),
        P("shot", None),
        P("shot", "tile"),
        P("shot", None, "tile"),
    )
    return jax.shard_map(
        per_device,
        mesh=mesh,
        in_specs=placed,
        out_specs=(
            P(None, "shot", "tile", None),
            P("shot", None, None, "tile", None),
            P("shot", None, None, "tile", None),
        ),
        check_vma=False,
    )
```

```python
import jax
import jax.numpy as jnp
from jax import lax
from jax.experimental import pallas as pl
from jax.experimental.pallas import tpu as pltpu
from jax.sharding import PartitionSpec as P

HALO = 12
OFF = 16
PADX = 8
INTERPRET = False


def d2(m2, m1, c0, p1, p2):
    return ((((-m2) + 16.0 * m1) - 30.0 * c0) + 16.0 * p1 - p2) * (1.0 / 12.0)


def place(dst, mid, lo, hi, at):
    w = lo.shape[-2]
    ax = mid.shape[-2]
    dst[..., pl.ds(at + OFF - w, w), :] = lo
    dst[..., pl.ds(at + OFF, ax), :] = mid
    dst[..., pl.ds(at + OFF + ax, w), :] = hi


def split3(x):
    hi = x.astype(jnp.bfloat16)
    lo = (x - hi.astype(jnp.float32)).astype(jnp.bfloat16)
    return hi, lo


def forward_kernel(wave_ref, fs_ref, sl_ref, sr_ref, tl_ref, tr_ref, co_ref, ch_ref, mask_ref, rrow_ref, rlane_ref,
                   h_ref, z_ref, rec_ref, pl_ref, q_ref, pb, qb, cf_ref, plocal, pickf):
    steps = h_ref.shape[0]
    az, xd, ay = mask_ref.shape
    ax = h_ref.shape[2]
    w = ch_ref.shape[2] // 2
    pb[...] = jnp.zeros(pb.shape, jnp.float32)
    qb[...] = jnp.zeros(qb.shape, jnp.float32)
    cf_ref[...] = jnp.zeros(cf_ref.shape, jnp.float32)
    inner = pl.ds(PADX, xd)
    place(pb.at[0, 2:2 + az], fs_ref[0], sl_ref[...], sr_ref[...], PADX)
    for k, (buf, slot) in enumerate(((qb, 0), (pb, 1), (qb, 1))):
        place(buf.at[slot, 2:2 + az], fs_ref[k + 1], tl_ref[k], tr_ref[k], PADX)
    place(cf_ref, co_ref[...], ch_ref[:, :, :w], ch_ref[:, :, w:], 0)
    lane = lax.broadcasted_iota(jnp.int32, (xd, ay), 1)
    n_rec = rrow_ref.shape[0]
    pickf[...] = jnp.where(lax.broadcasted_iota(jnp.int32, pickf.shape, 1) == rrow_ref[...], 1.0, 0.0).astype(jnp.bfloat16)
    for n in range(steps):
        cur = n % 2
        old = 1 - cur
        wv = wave_ref[n]

        def plane(d, carry):
            pc = pb[cur, d + 2, inner, :]
            d2x = d2(pb[cur, d + 2, pl.ds(PADX - 2, xd), :], pb[cur, d + 2, pl.ds(PADX - 1, xd), :], pc,
                     pb[cur, d + 2, pl.ds(PADX + 1, xd), :], pb[cur, d + 2, pl.ds(PADX + 2, xd), :])
            ym2 = jnp.where(lane >= 2, pltpu.roll(pc, 2, 1), 0.0)
            ym1 = jnp.where(lane >= 1, pltpu.roll(pc, 1, 1), 0.0)
            yp1 = jnp.where(lane < ay - 1, pltpu.roll(pc, ay - 1, 1), 0.0)
            yp2 = jnp.where(lane < ay - 2, pltpu.roll(pc, ay - 2, 1), 0.0)
            h = d2x + d2(ym2, ym1, pc, yp1, yp2)
            qc = qb[cur, d + 2, inner, :]
            z = d2(qb[cur, d, inner, :], qb[cur, d + 1, inner, :], qc, qb[cur, d + 3, inner, :], qb[cur, d + 4, inner, :])
            c = cf_ref[0, d]
            a = cf_ref[1, d]
            b = cf_ref[2, d]
            pulse = wv * mask_ref[d]
            pn = 2.0 * pc - pb[old, d + 2, inner, :] + c * (a * h + b * z) + pulse
            qn = 2.0 * qc - qb[old, d + 2, inner, :] + c * (b * h + z) + pulse
            pb[old, d + 2, inner, :] = pn
            qb[old, d + 2, inner, :] = qn
            h_ref[n, d] = h[OFF:OFF + ax]
            z_ref[n, d] = z[OFF:OFF + ax]
            po = pn[OFF:OFF + ax]
            plocal[pl.ds(pl.multiple_of(d * ax, ax), ax), :] = po
            if n == steps - 1:
                q_ref[d] = qn[OFF:OFF + ax]
                pl_ref[d] = po
            return carry

        lax.fori_loop(0, az, plane, 0)
        got = None
        for part in split3(plocal[...]):
            term = jnp.dot(pickf[...], part, preferred_element_type=jnp.float32)
            got = term if got is None else got + term
        sel = lax.broadcasted_iota(jnp.int32, (n_rec, ay), 1) == rlane_ref[...]
        rec_ref[n] = jnp.where(sel, got, 0.0)


def adjoint_kernel(ad_ref, al_ref, ar_ref, bl_ref, br_ref, co_ref, ch_ref, h_ref, z_ref, row_ref, m_ref, acc_ref, fin_ref, lb, mb, ob, fb, cf_ref):
    steps = h_ref.shape[0]
    az, xd, ay = ob.shape[0] - 4, ob.shape[1], ob.shape[2]
    ax = h_ref.shape[2]
    w = ch_ref.shape[2] // 2
    lb[...] = jnp.zeros(lb.shape, jnp.float32)
    mb[...] = jnp.zeros(mb.shape, jnp.float32)
    cf_ref[...] = jnp.zeros(cf_ref.shape, jnp.float32)
    for k, (buf, slot) in enumerate(((lb, 0), (mb, 0))):
        place(buf.at[slot], ad_ref[k], al_ref[k], ar_ref[k], 0)
    for k, (buf, slot) in enumerate(((lb, 1), (mb, 1))):
        place(buf.at[slot], ad_ref[k + 2], bl_ref[k], br_ref[k], 0)
    place(cf_ref, co_ref[...], ch_ref[:, :, :w], ch_ref[:, :, w:], 0)
    ob[...] = jnp.zeros(ob.shape, jnp.float32)
    fb[...] = jnp.zeros(fb.shape, jnp.float32)
    acc_ref[...] = jnp.zeros(acc_ref.shape, jnp.float32)
    lane = lax.broadcasted_iota(jnp.int32, (xd, ay), 1)
    inner = pl.ds(PADX, xd)
    for s in reversed(range(steps)):
        cur = (steps - 1 - s) % 2
        old = 1 - cur

        def other_plane(d, carry):
            ob[d + 2] = cf_ref[0, d] * (cf_ref[2, d] * lb[cur, d] + mb[cur, d])
            return carry

        lax.fori_loop(0, az, other_plane, 0)

        def plane(d, carry):
            lc = lb[cur, d]
            mc = mb[cur, d]
            c = cf_ref[0, d]
            a = cf_ref[1, d]
            b = cf_ref[2, d]
            f = c * (a * lc + b * mc)
            fb[inner, :] = f
            d2x = d2(fb[pl.ds(PADX - 2, xd), :], fb[pl.ds(PADX - 1, xd), :], f, fb[pl.ds(PADX + 1, xd), :], fb[pl.ds(PADX + 2, xd), :])
            ym2 = jnp.where(lane >= 2, pltpu.roll(f, 2, 1), 0.0)
            ym1 = jnp.where(lane >= 1, pltpu.roll(f, 1, 1), 0.0)
            yp1 = jnp.where(lane < ay - 1, pltpu.roll(f, ay - 1, 1), 0.0)
            yp2 = jnp.where(lane < ay - 2, pltpu.roll(f, ay - 2, 1), 0.0)
            hf = d2x + d2(ym2, ym1, f, yp1, yp2)
            hit = lax.broadcasted_iota(jnp.int32, (xd, row_ref.shape[1]), 0) + d * xd == row_ref[...]
            pick = jnp.where(hit, 1.0, 0.0).astype(jnp.bfloat16)
            e = jnp.dot(pick, m_ref[s, 0], preferred_element_type=jnp.float32)
            e = e + jnp.dot(pick, m_ref[s, 1], preferred_element_type=jnp.float32)
            ln = e + 2.0 * lc + hf - lb[old, d]
            mn = 2.0 * mc + d2(ob[d], ob[d + 1], ob[d + 2], ob[d + 3], ob[d + 4]) - mb[old, d]
            lb[old, d] = ln
            mb[old, d] = mn
            lo = ln[OFF:OFF + ax]
            mo = mn[OFF:OFF + ax]
            h = h_ref[s, d]
            z = z_ref[s, d]
            acc_ref[0, d] = acc_ref[0, d] + lo * h
            acc_ref[1, d] = acc_ref[1, d] + lo * z + mo * h
            acc_ref[2, d] = acc_ref[2, d] + mo * z
            if s == 0:
                fin_ref[0, d] = lo
                fin_ref[1, d] = mo
            return carry

        lax.fori_loop(0, az, plane, 0)


def run_adjoint(ad, al, ar, bl, br, co, ch, h_all, z_all, row, parts):
    _, az, ax, ay = ad.shape
    xd = ax + 2 * OFF
    vm = pl.BlockSpec(memory_space=pltpu.VMEM)
    return pl.pallas_call(
        adjoint_kernel,
        out_shape=(jax.ShapeDtypeStruct((3, az, ax, ay), jnp.float32), jax.ShapeDtypeStruct((2, az, ax, ay), jnp.float32)),
        in_specs=[vm] * 11,
        out_specs=(vm, vm),
        scratch_shapes=[
            pltpu.VMEM((2, az, xd, ay), jnp.float32),
            pltpu.VMEM((2, az, xd, ay), jnp.float32),
            pltpu.VMEM((az + 4, xd, ay), jnp.float32),
            pltpu.VMEM((xd + 2 * PADX, ay), jnp.float32),
            pltpu.VMEM((3, az, xd, ay), jnp.float32),
        ],
        compiler_params=pltpu.CompilerParams(vmem_limit_bytes=62 * 1024 * 1024),
        interpret=INTERPRET,
    )(ad, al, ar, bl, br, co, ch, h_all, z_all, row, parts)


def exact_parts(x):
    hi = lax.reduce_precision(x, exponent_bits=8, mantissa_bits=7)
    rest = x - hi
    lo = lax.reduce_precision(rest, exponent_bits=8, mantissa_bits=7)
    return hi.astype(jnp.bfloat16), lo.astype(jnp.bfloat16)


def run_forward(wave, fs, sl, sr, tl, tr, co, ch, mask, rrow, rlane):
    steps = wave.shape[0]
    az, xd, ay = mask.shape
    ax = fs.shape[2]
    n_rec = rrow.shape[0]
    vm = pl.BlockSpec(memory_space=pltpu.VMEM)
    loc = jax.ShapeDtypeStruct((steps, az, ax, ay), jnp.float32)
    one = jax.ShapeDtypeStruct((az, ax, ay), jnp.float32)
    return pl.pallas_call(
        forward_kernel,
        out_shape=(loc, loc, jax.ShapeDtypeStruct((steps, n_rec, ay), jnp.float32), one, one),
        in_specs=[pl.BlockSpec(memory_space=pltpu.SMEM)] + [vm] * 10,
        out_specs=(vm, vm, vm, vm, vm),
        scratch_shapes=[pltpu.VMEM((2, az + 4, xd + 2 * PADX, ay), jnp.float32)] * 2
        + [pltpu.VMEM((3, az, xd, ay), jnp.float32), pltpu.VMEM((az * ax, ay), jnp.float32),
           pltpu.VMEM((n_rec, az * ax), jnp.bfloat16)],
        compiler_params=pltpu.CompilerParams(vmem_limit_bytes=62 * 1024 * 1024),
        interpret=INTERPRET,
    )(wave, fs, sl, sr, tl, tr, co, ch, mask, rrow, rlane)


def taps(padded, size, axis):

    def part(k):
        return lax.slice_in_dim(padded, k, k + size, axis=axis)

    return (-part(0) + 16.0 * part(1) - 30.0 * part(2) + 16.0 * part(3) - part(4)) / 12.0


def along_local(field, axis):
    pads = [(0, 0)] * field.ndim
    pads[axis] = (2, 2)
    return taps(jnp.pad(field, pads), field.shape[axis], axis)


def horiz(field):
    return along_local(field, field.ndim - 2) + along_local(field, field.ndim - 1)


def to_left_right(head, tail, axis):
    count = lax.axis_size(axis)
    from_left = lax.ppermute(tail, axis, [(i, i + 1) for i in range(count - 1)])
    from_right = lax.ppermute(head, axis, [(i + 1, i) for i in range(count - 1)])
    return from_left, from_right


def rows(x):
    return x.reshape(-1, x.shape[-1])


def per_device(coefs, fwd_state, adj_state, src_cell, src_wave, rec_cells, observed):
    w = HALO
    _, zl, ax, ay = coefs.shape
    n_tile = lax.axis_size("tile")
    tile = lax.axis_index("tile")
    steps = src_wave.shape[1]
    full = lax.all_gather(coefs, "shot", axis=1, tiled=True)
    az = full.shape[1]
    xe = ax + 2 * OFF
    ext_shape = (az, xe, ay)
    cells_ext = az * xe * ay

    def widen(lo, mid, hi):
        pad = jnp.zeros(mid.shape[:-2] + (OFF - w, ay), jnp.float32)
        lo, hi = lax.optimization_barrier((jnp.concatenate([pad, lo], axis=-2), jnp.concatenate([hi, pad], axis=-2)))
        return jnp.concatenate([lo, mid, hi], axis=-2)

    fs = fwd_state[0]
    src_row = jnp.broadcast_to(src_cell[0, 0].astype(jnp.float32), (1, ay))
    v = w - 2
    head1 = jnp.concatenate([rows(fs[0, :, :w]), rows(fs[1:, :, :v]), rows(coefs[:, :, :w]), src_row], axis=0)
    tail1 = jnp.concatenate([rows(fs[0, :, ax - w:]), rows(fs[1:, :, ax - v:]), rows(coefs[:, :, ax - w:]), src_row], axis=0)
    left1, right1 = to_left_right(head1, tail1, "tile")
    n_p = az * w
    n_o = 3 * az * v
    n_cf = 3 * zl * w

    def unpack1(m):
        sp = m[:n_p].reshape(az, w, ay)
        so = m[n_p:n_p + n_o].reshape(3, az, v, ay)
        cf = m[n_p + n_o:n_p + n_o + n_cf].reshape(3, zl, w, ay)
        sc = m[n_p + n_o + n_cf, 0]
        return sp, so, cf, sc

    sp_l, so_l, cf_l, sc_l = unpack1(left1)
    sp_r, so_r, cf_r, sc_r = unpack1(right1)
    cf_halo = lax.all_gather(jnp.concatenate([cf_l, cf_r], axis=2), "shot", axis=1, tiled=True)

    def ext_index(cell, shift):
        depth = cell // (ax * ay)
        first = (cell // ay) % ax + shift + OFF
        second = cell % ay
        ok = (first >= OFF - w) & (first < xe - OFF + w)
        return jnp.where(ok, (depth * xe + first) * ay + second, cells_ext), ok

    src_own, _ = ext_index(src_cell[0, 0], 0)
    src_lft, ok_l = ext_index(sc_l.astype(jnp.int32), -ax)
    src_rgt, ok_r = ext_index(sc_r.astype(jnp.int32), ax)
    ok_l = ok_l & (tile > 0)
    ok_r = ok_r & (tile < n_tile - 1)
    src_idx = jnp.stack([src_own, src_lft, src_rgt])
    src_on = jnp.stack([jnp.float32(1.0), ok_l.astype(jnp.float32), ok_r.astype(jnp.float32)])
    source_mask = jnp.zeros((cells_ext,), jnp.float32).at[src_idx].add(src_on, mode="drop").reshape(ext_shape)

    ad = adj_state[0]
    ad_head = jnp.concatenate([rows(ad[:2, :, :w]), rows(ad[2:, :, :v])], axis=0)
    ad_tail = jnp.concatenate([rows(ad[:2, :, ax - w:]), rows(ad[2:, :, ax - v:])], axis=0)
    ad_head, ad_tail, sp_l, sp_r = lax.optimization_barrier((ad_head, ad_tail, sp_l, sp_r))
    left2, right2 = to_left_right(ad_head, ad_tail, "tile")
    n_a = 2 * az * w

    def unpack2(m):
        return m[:n_a].reshape(2, az, w, ay), m[n_a:].reshape(2, az, v, ay)

    al, bl = unpack2(left2)
    ar, br = unpack2(right2)

    receivers = rec_cells[0]
    h_all, z_all, rec_mat, p_last, q_last = run_forward(
        src_wave[0], fs, sp_l, sp_r, so_l, so_r, full, cf_halo, source_mask, (receivers // ay)[:, None], (receivers % ay)[:, None])
    records = jnp.sum(rec_mat, axis=2) - observed[0]

    msg = jnp.concatenate([records, receivers.astype(jnp.float32)[None]], axis=0)
    left3, right3 = to_left_right(msg, msg, "tile")
    rec_own, _ = ext_index(receivers, 0)
    rec_l, okr_l = ext_index(left3[steps].astype(jnp.int32), -ax)
    rec_r, okr_r = ext_index(right3[steps].astype(jnp.int32), ax)
    okr_l = okr_l & (tile > 0)
    okr_r = okr_r & (tile < n_tile - 1)
    rec_l = jnp.where(okr_l, rec_l, cells_ext)
    rec_r = jnp.where(okr_r, rec_r, cells_ext)
    rec_all = jnp.concatenate([rec_own, rec_l, rec_r])

    pick_lane = lax.broadcasted_iota(jnp.int32, (rec_all.shape[0], ay), 1) == (rec_all % ay)[:, None]
    parts = []
    for step in range(steps):
        vals = jnp.concatenate([records[step], left3[step], right3[step]])
        parts.append(jnp.stack(exact_parts(jnp.where(pick_lane, vals[:, None], 0.0))))
    rec_rows = (rec_all // ay)[None, :]
    acc, fin = run_adjoint(ad, al, ar, bl, br, full, cf_halo, h_all, z_all, rec_rows, jnp.stack(parts))

    n_shot = lax.axis_size("shot")
    n_y = n_shot // 2
    zc = az // n_shot
    me = lax.axis_index("shot")
    core = me % 2
    yy = me // 2
    chunks = acc.reshape(3, n_y, 2, zc, ax, ay)
    send = lax.dynamic_index_in_dim(chunks, 1 - core, axis=2, keepdims=False)
    got = lax.ppermute(send, "shot", [(i, i ^ 1) for i in range(n_shot)])
    mine = lax.dynamic_index_in_dim(chunks, core, axis=2, keepdims=False) + got
    ring = [(y * 2 + c, ((y + 1) % n_y) * 2 + c) for y in range(n_y) for c in range(2)]
    partial = lax.dynamic_index_in_dim(mine, (yy + n_y - 1) % n_y, axis=1, keepdims=False)
    for t in range(n_y - 1):
        partial = lax.ppermute(partial, "shot", ring)
        partial = partial + lax.dynamic_index_in_dim(mine, (yy + 2 * n_y - t - 2) % n_y, axis=1, keepdims=False)
    summed = partial
    q_h, q_x, q_z = summed[0], summed[1], summed[2]
    c, a, b = coefs[0], coefs[1], coefs[2]
    gradient = jnp.stack([a * q_h + b * q_x + q_z, c * q_h, c * q_x])
    fwd_final = jnp.stack([p_last, q_last])[None]
    adj_final = fin[None]
    return (gradient, fwd_final, adj_final)


def solution(mesh):
    placed = (
        P(None, "shot", "tile", None),
        P("shot", None, None, "tile", None),
        P("shot", None, None, "tile", None),
        P("shot", "tile"),
        P("shot", None),
        P("shot", "tile"),
        P("shot", None, "tile"),
    )
    return jax.shard_map(
        per_device,
        mesh=mesh,
        in_specs=placed,
        out_specs=(
            P(None, "shot", "tile", None),
            P("shot", None, None, "tile", None),
            P("shot", None, None, "tile", None),
        ),
        check_vma=False,
    )
```
